256 devices in a mesh: proto: 4 (over y), batch: 64 (over x, z, core).
Axes of the slice: x: 4, y: 4, z: 8, core: 2. Of those that a mesh axis runs over, the one named last changes fastest.
Arguments:
- teacher: bfloat16 [32768, 256], P(('proto', 'batch')), may hold values from -6 to 6
- student: bfloat16 [32768, 256], P(('proto', 'batch')), may hold values from -6 to 6
- prototypes: bfloat16 [32768, 256], P('proto'), may hold values from -6 to 6
Outputs:
- grad_student: float32 [32768, 256], P(('proto', 'batch'))
- grad_protos: float32 [32768, 256], P(('proto', 'batch'))
The draws below stay inside these ranges and needn't reach their ends.
All inputs are finite; a program needn't handle non-finite values.
Results may differ from the reference program's by a relative error of at most 0.0042.
Values may be sent and summed in bfloat16 or wider, within the bound.
No kernel may reach another device: no remote copies, remote signals or barrier semaphores. Data moves between devices by JAX's collectives and lax.ppermute only.
A program may use at most 192 MiB of HBM per device.

```python
import math
import jax
import jax.numpy as jnp
from jax import lax

D = 256
ITERS = 3
K = 32768
B = 32768


def block_levels(stream_key, shape, cuts, least, top_value):
    gain = 1.0
    for axis_at, shards_of in cuts:
        heights = jax.random.uniform(jax.random.fold_in(jax.random.fold_in(stream_key, 6), axis_at), (shards_of,), jnp.float32, least / len(cuts), top_value / len(cuts))
        gain = gain * jnp.repeat(jnp.exp(heights), shape[axis_at] // shards_of).reshape((-1,) + (1,) * (len(shape) - 1 - axis_at))
    return gain


def centred(stream_key, extent, scale, reach, pieces=(), kind=jnp.bfloat16):
    loudness = block_levels(stream_key, extent, pieces, -0.22, 0.18) if pieces else 1.0
    entries = jax.random.normal(stream_key, extent, jnp.float32) * scale * loudness
    return jnp.minimum(jnp.maximum(entries, -reach), reach).astype(kind)


def setup_inputs(seed: int = 0) -> dict:
    key_of = jax.random.split(jax.random.key(seed), 4)
    teacher = centred(key_of[0], (B, D), 1.0, 6.0, ((0, 256),))
    student = centred(key_of[1], (B, D), 1.0, 6.0, ((0, 256),))
    prototypes = centred(key_of[2], (K, D), 1.0, 6.0, ((0, 4),))
    return dict(teacher=teacher, student=student, prototypes=prototypes)


teacher_temp = 0.05
student_temp = 0.1

def unit_rows(value):
    full = value.astype(jnp.float32)
    return full * lax.rsqrt(lax.optimization_barrier(jnp.mean(full * full, axis=1, keepdims=True)) + 1e-06) / math.sqrt(value.shape[1])

def against(left, right):
    return lax.dot_general(left, right, (((1,), (1,)), ((), ())), preferred_element_type=jnp.float32)

def reference(teacher, student, prototypes):
    tn = unit_rows(teacher).astype(jnp.bfloat16)
    sn = unit_rows(student).astype(jnp.bfloat16)
    cn = unit_rows(prototypes).astype(jnp.bfloat16)
    rows, width = teacher.shape
    count = prototypes.shape[0]
    block = math.gcd(rows, 1024)
    nblocks = rows // block
    t_blocks = tn.reshape(nblocks, block, width)
    s_blocks = sn.reshape(nblocks, block, width)

    def weights(tblock):
        return jnp.exp(against(tblock, cn) / teacher_temp)

    def first(mass, tblock):
        return (mass + lax.optimization_barrier(jnp.sum(weights(tblock), axis=0)), None)
    mass, _ = lax.scan(first, jnp.zeros((count,), jnp.float32), t_blocks)
    col = 1.0 / (count * mass)
    row_blocks = None
    for step in range(ITERS):

        def sweep(mass_acc, tblock, col=col):
            weight = weights(tblock)
            rowf = 1.0 / (rows * lax.optimization_barrier(jnp.sum(weight * col[None, :], axis=1)))
            return (mass_acc + lax.optimization_barrier(jnp.sum(weight * rowf[:, None], axis=0)), rowf)
        mass, row_blocks = lax.scan(sweep, jnp.zeros((count,), jnp.float32), t_blocks)
        if step < ITERS - 1:
            col = 1.0 / (count * mass)
    scale = 16.0 * math.sqrt(count)

    def final(gproto, items):
        tblock, sblock, rowf = items
        target = rows * weights(tblock) * rowf[:, None] * col[None, :]
        logits = against(sblock, cn) / student_temp
        logz = jnp.log(lax.optimization_barrier(jnp.sum(jnp.exp(logits), axis=1)))
        logp = logits - logz[:, None]
        grads = (scale * (jnp.exp(logp) - target)).astype(jnp.bfloat16)
        gsess = jnp.dot(grads, cn, preferred_element_type=jnp.float32) / student_temp
        gproto = gproto + lax.dot_general(grads, sblock, (((0,), (0,)), ((), ())), preferred_element_type=jnp.float32) / student_temp
        return (gproto, gsess)
    gproto, gsess = lax.scan(final, jnp.zeros((count, width), jnp.float32), (t_blocks, s_blocks, row_blocks))
    gsess = gsess.reshape(rows, width)
    _, pull = jax.vjp(unit_rows, student.astype(jnp.float32))
    grad_student = pull(gsess)[0]
    return (grad_student, gproto)
```

```python
import math

import jax
import jax.numpy as jnp
from jax import lax
from jax.sharding import PartitionSpec as P

ITERS = 3


teacher_temp = 0.05
student_temp = 0.1


def side_by_side(arrays, axis, dim, along):
    ends, at = ([], 0)
    for a in arrays[:-1]:
        at += a.shape[along]
        ends.append(at)
    both = jnp.concatenate(arrays, axis=along)
    return tuple(jnp.split(lax.all_gather(both, axis, axis=dim, tiled=True), ends, axis=along))


def unit_rows(value):
    full = value.astype(jnp.float32)
    return (
        full
        * lax.rsqrt(jnp.mean(full * full, axis=1, keepdims=True) + 1e-06)
        / math.sqrt(value.shape[1])
    )


def against(left, right):
    return lax.dot_general(
        left, right, (((1,), (1,)), ((), ())), preferred_element_type=jnp.float32
    )


def per_device(teacher, student, prototypes):
    n_proto = lax.axis_size("proto")
    n_batch = lax.axis_size("batch")
    own_rows = teacher.shape[0]
    count_all = prototypes.shape[0] * n_proto
    rows_all = own_rows * n_proto * n_batch
    tn = unit_rows(teacher).astype(jnp.bfloat16)
    sn = unit_rows(student).astype(jnp.bfloat16)
    cn = unit_rows(prototypes).astype(jnp.bfloat16)
    tn_group, sn_group = side_by_side((tn, sn), "proto", 0, 1)
    weight = jnp.exp(against(tn_group, cn) / teacher_temp)
    row_scale = jnp.ones((tn_group.shape[0],), jnp.float32)
    col_scale = None
    for step in range(ITERS):
        mass_local = jnp.sum(weight * row_scale[:, None], axis=0)
        col_scale = 1.0 / (count_all * lax.psum(mass_local, "batch"))
        sample_local = jnp.sum(weight * col_scale[None, :], axis=1)
        row_scale = 1.0 / (rows_all * lax.psum(sample_local, "proto"))
    targets = rows_all * weight * row_scale[:, None] * col_scale[None, :]
    logits = against(sn_group, cn) / student_temp
    logz = jnp.log(lax.psum(jnp.sum(jnp.exp(logits), axis=1), "proto"))
    logp = logits - logz[:, None]
    scale = 16.0 * math.sqrt(count_all)
    grads = (scale * (jnp.exp(logp) - targets)).astype(jnp.bfloat16)
    grad_sn = lax.psum_scatter(
        jnp.dot(grads, cn, preferred_element_type=jnp.float32) / student_temp,
        "proto",
        scatter_dimension=0,
        tiled=True,
    )
    _, pull = jax.vjp(unit_rows, student.astype(jnp.float32))
    grad_student = pull(grad_sn)[0]
    proto_partial = (
        lax.dot_general(
            grads, sn_group, (((0,), (0,)), ((), ())), preferred_element_type=jnp.float32
        )
        / student_temp
    )
    grad_protos = lax.psum_scatter(proto_partial, "batch", scatter_dimension=0, tiled=True)
    return (grad_student, grad_protos)


def solution(mesh):
    return jax.shard_map(
        per_device,
        mesh=mesh,
        in_specs=(P(("proto", "batch"), None), P(("proto", "batch"), None), P("proto", None)),
        out_specs=(P(("proto", "batch"), None), P(("proto", "batch"), None)),
        check_vma=False,
    )
```

```python
import math

import jax
import jax.numpy as jnp
from jax import lax
from jax.sharding import PartitionSpec as P

ITERS = 3


teacher_temp = 0.05
student_temp = 0.1


def side_by_side(arrays, axis, dim, along):
    ends, at = ([], 0)
    for a in arrays[:-1]:
        at += a.shape[along]
        ends.append(at)
    both = jnp.concatenate(arrays, axis=along)
    return tuple(jnp.split(lax.all_gather(both, axis, axis=dim, tiled=True), ends, axis=along))


def cut_along(value, dim, length):
    lengths = value.shape
    parts = value.reshape(*lengths[:dim], length, lengths[dim] // length, *lengths[dim + 1 :])
    return jnp.moveaxis(parts, dim, 0)


def summed_on_arrival(value, axis, dim):
    parts = cut_along(value, dim, lax.axis_size(axis))
    arrived = lax.all_to_all(parts, axis, split_axis=0, concat_axis=0, tiled=True)
    return arrived.sum(axis=0)


def laid_out(parts, dim):
    parts = jnp.moveaxis(parts, 0, dim)
    lengths = parts.shape
    return parts.reshape(*lengths[:dim], lengths[dim] * lengths[dim + 1], *lengths[dim + 2 :])


def copy_for_each(value, axis):
    copies = jnp.broadcast_to(value, (lax.axis_size(axis), *value.shape))
    return lax.all_to_all(copies, axis, split_axis=0, concat_axis=0, tiled=True)


def gather_directly(value, axis, dim):
    return laid_out(copy_for_each(value, axis), dim)


def over_copies(value, axis):
    return copy_for_each(value, axis).sum(axis=0)


def gather_turned(arrays, axis, dims):
    turned = [jnp.moveaxis(a, dim, 0) for a, dim in zip(arrays, dims)]
    widths = [t[0].size for t in turned]
    both = jnp.concatenate([t.reshape(-1, w) for t, w in zip(turned, widths)], axis=1)
    out = lax.all_gather(both, axis, axis=0, tiled=True)
    parts = jnp.split(out, [sum(widths[:k]) for k in range(1, len(widths))], axis=1)
    return tuple(
        (
            jnp.moveaxis(b.reshape(-1, *t.shape[1:]), 0, dim)
            for b, t, dim in zip(parts, turned, dims)
        )
    )


def unit_rows(value):
    full = value.astype(jnp.float32)
    return (
        full
        * lax.rsqrt(jnp.mean(full * full, axis=1, keepdims=True) + 1e-06)
        / math.sqrt(value.shape[1])
    )


def against(left, right):
    return lax.dot_general(
        left, right, (((1,), (1,)), ((), ())), preferred_element_type=jnp.float32
    )


def per_device(teacher, student, prototypes):
    n_proto = lax.axis_size("proto")
    n_batch = lax.axis_size("batch")
    own_rows = teacher.shape[0]
    count_all = prototypes.shape[0] * n_proto
    rows_all = own_rows * n_proto * n_batch
    tn = unit_rows(teacher).astype(jnp.bfloat16)
    sn = unit_rows(student).astype(jnp.bfloat16)
    cn = unit_rows(prototypes).astype(jnp.bfloat16)
    tn_group, sn_group = side_by_side((tn, sn), "proto", 0, 1)
    weight = jnp.exp(against(tn_group, cn) / teacher_temp)
    row_scale = jnp.ones((tn_group.shape[0],), jnp.float32)
    col_scale = None
    for step in range(ITERS):
        mass_local = jnp.sum(weight * row_scale[:, None], axis=0)
        share = summed_on_arrival(mass_local, "batch", 0)
        col_scale = gather_directly(1.0 / (count_all * share), "batch", 0)
        sample_local = jnp.sum(weight * col_scale[None, :], axis=1)
        row_scale = 1.0 / (rows_all * over_copies(sample_local, "proto"))
    targets = rows_all * weight * row_scale[:, None] * col_scale[None, :]
    logits = against(sn_group, cn) / student_temp
    logz = jnp.log(over_copies(jnp.sum(jnp.exp(logits), axis=1), "proto"))
    logp = logits - logz[:, None]
    scale = 16.0 * math.sqrt(count_all)
    grads = (scale * (jnp.exp(logp) - targets)).astype(jnp.bfloat16)
    grad_sn = summed_on_arrival(
        jnp.dot(grads, cn, preferred_element_type=jnp.float32) / student_temp, "proto", 0
    )
    _, pull = jax.vjp(unit_rows, student.astype(jnp.float32))
    grad_student = pull(grad_sn)[0]
    mine_rows = prototypes.shape[0] // n_batch
    offset = lax.axis_index("batch") * mine_rows
    c_mine = lax.dynamic_slice_in_dim(cn, offset, mine_rows, 0)
    col_mine = lax.dynamic_slice_in_dim(col_scale, offset, mine_rows, 0)
    both = gather_directly(jnp.stack([row_scale, logz], axis=1), "batch", 0)
    all_scale, all_logz = both[:, 0], both[:, 1]
    t_piece, s_piece = side_by_side((tn_group, sn_group), "batch", 0, 1)
    target = (
        rows_all
        * jnp.exp(against(t_piece, c_mine) / teacher_temp)
        * all_scale[:, None]
        * col_mine[None, :]
    )
    probs = jnp.exp(against(s_piece, c_mine) / student_temp - all_logz[:, None])
    local_grads = (scale * (probs - target)).astype(jnp.bfloat16)
    grad_protos = (
        lax.dot_general(
            local_grads, s_piece, (((0,), (0,)), ((), ())), preferred_element_type=jnp.float32
        )
        / student_temp
    )
    return (grad_student, grad_protos)


def solution(mesh):
    return jax.shard_map(
        per_device,
        mesh=mesh,
        in_specs=(P(("proto", "batch"), None), P(("proto", "batch"), None), P("proto", None)),
        out_specs=(P(("proto", "batch"), None), P(("proto", "batch"), None)),
        check_vma=False,
    )
```

```python
import math

import jax
import jax.numpy as jnp
from jax import lax
from jax.sharding import PartitionSpec as P
from jax.experimental import pallas as pl
from jax.experimental.pallas import tpu as pltpu
import functools

ITERS = 3


teacher_temp = 0.05
student_temp = 0.1

def _protos_kernel(ts_ref, c_ref, col_ref, al_ref, out_ref, *, rows_all, scale, width):
    @pl.when(pl.program_id(0) == 0)
    def _():
        out_ref[...] = jnp.zeros_like(out_ref)

    t = ts_ref[:, :width]
    s = ts_ref[:, width:]
    c = c_ref[...]
    dims = (((1,), (1,)), ((), ()))
    tl = lax.dot_general(c, t, dims, preferred_element_type=jnp.float32)
    sl = lax.dot_general(c, s, dims, preferred_element_type=jnp.float32)
    a = al_ref[0:1, :]
    logz = al_ref[1:2, :]
    target = rows_all * jnp.exp(tl / teacher_temp) * a * col_ref[...]
    probs = jnp.exp(sl / student_temp - logz)
    g = (scale * (probs - target)).astype(jnp.bfloat16)
    out_ref[...] += jnp.dot(g, s, preferred_element_type=jnp.float32)


def protos_grad(ts, c_mine, col_mine, al, rows_all, scale, block=2048, interpret=False):
    n, w2 = ts.shape
    width = w2 // 2
    m = c_mine.shape[0]
    kern = functools.partial(_protos_kernel, rows_all=rows_all, scale=scale, width=width)
    out = pl.pallas_call(
        kern,
        grid=(n // block,),
        in_specs=[
            pl.BlockSpec((block, w2), lambda i: (i, 0)),
            pl.BlockSpec((m, width), lambda i: (0, 0)),
            pl.BlockSpec((m, 1), lambda i: (0, 0)),
            pl.BlockSpec((2, block), lambda i: (0, i)),
        ],
        out_specs=pl.BlockSpec((m, width), lambda i: (0, 0)),
        out_shape=jax.ShapeDtypeStruct((m, width), jnp.float32),
        compiler_params=pltpu.CompilerParams(dimension_semantics=("arbitrary",)),
        interpret=interpret,
    )(ts, c_mine, col_mine.reshape(m, 1), al)
    return out / student_temp


def side_by_side(arrays, axis, dim, along):
    ends, at = ([], 0)
    for a in arrays[:-1]:
        at += a.shape[along]
        ends.append(at)
    both = jnp.concatenate(arrays, axis=along)
    return tuple(jnp.split(lax.all_gather(both, axis, axis=dim, tiled=True), ends, axis=along))


def cut_along(value, dim, length):
    lengths = value.shape
    parts = value.reshape(*lengths[:dim], length, lengths[dim] // length, *lengths[dim + 1 :])
    return jnp.moveaxis(parts, dim, 0)


def summed_on_arrival(value, axis, dim):
    parts = cut_along(value, dim, lax.axis_size(axis))
    arrived = lax.all_to_all(parts, axis, split_axis=0, concat_axis=0, tiled=True)
    return arrived.sum(axis=0)


def laid_out(parts, dim):
    parts = jnp.moveaxis(parts, 0, dim)
    lengths = parts.shape
    return parts.reshape(*lengths[:dim], lengths[dim] * lengths[dim + 1], *lengths[dim + 2 :])


def copy_for_each(value, axis):
    copies = jnp.broadcast_to(value, (lax.axis_size(axis), *value.shape))
    return lax.all_to_all(copies, axis, split_axis=0, concat_axis=0, tiled=True)


def gather_directly(value, axis, dim):
    return laid_out(copy_for_each(value, axis), dim)


def over_copies(value, axis):
    return copy_for_each(value, axis).sum(axis=0)


def gather_turned(arrays, axis, dims):
    turned = [jnp.moveaxis(a, dim, 0) for a, dim in zip(arrays, dims)]
    widths = [t[0].size for t in turned]
    both = jnp.concatenate([t.reshape(-1, w) for t, w in zip(turned, widths)], axis=1)
    out = lax.all_gather(both, axis, axis=0, tiled=True)
    parts = jnp.split(out, [sum(widths[:k]) for k in range(1, len(widths))], axis=1)
    return tuple(
        (
            jnp.moveaxis(b.reshape(-1, *t.shape[1:]), 0, dim)
            for b, t, dim in zip(parts, turned, dims)
        )
    )


def unit_rows(value):
    full = value.astype(jnp.float32)
    return (
        full
        * lax.rsqrt(jnp.mean(full * full, axis=1, keepdims=True) + 1e-06)
        / math.sqrt(value.shape[1])
    )


def against(left, right):
    return lax.dot_general(
        left, right, (((1,), (1,)), ((), ())), preferred_element_type=jnp.float32
    )


def per_device(teacher, student, prototypes):
    n_proto = lax.axis_size("proto")
    n_batch = lax.axis_size("batch")
    own_rows = teacher.shape[0]
    count_all = prototypes.shape[0] * n_proto
    rows_all = own_rows * n_proto * n_batch
    tn = unit_rows(teacher).astype(jnp.bfloat16)
    sn = unit_rows(student).astype(jnp.bfloat16)
    cn = unit_rows(prototypes).astype(jnp.bfloat16)
    tn_group, sn_group = side_by_side((tn, sn), "proto", 0, 1)
    weight = jnp.exp(against(tn_group, cn) / teacher_temp)
    row_scale = jnp.ones((tn_group.shape[0],), jnp.float32)
    col_scale = None
    for step in range(ITERS):
        mass_local = jnp.sum(weight * row_scale[:, None], axis=0)
        share = summed_on_arrival(mass_local, "batch", 0)
        col_scale = gather_directly(1.0 / (count_all * share), "batch", 0)
        sample_local = jnp.sum(weight * col_scale[None, :], axis=1)
        row_scale = 1.0 / (rows_all * over_copies(sample_local, "proto"))
    targets = rows_all * weight * row_scale[:, None] * col_scale[None, :]
    logits = against(sn_group, cn) / student_temp
    logz = jnp.log(over_copies(jnp.sum(jnp.exp(logits), axis=1), "proto"))
    logp = logits - logz[:, None]
    scale = 16.0 * math.sqrt(count_all)
    grads = (scale * (jnp.exp(logp) - targets)).astype(jnp.bfloat16)
    grad_sn = summed_on_arrival(
        jnp.dot(grads, cn, preferred_element_type=jnp.float32) / student_temp, "proto", 0
    )
    _, pull = jax.vjp(unit_rows, student.astype(jnp.float32))
    grad_student = pull(grad_sn)[0]
    mine_rows = prototypes.shape[0] // n_batch
    offset = lax.axis_index("batch") * mine_rows
    c_mine = lax.dynamic_slice_in_dim(cn, offset, mine_rows, 0)
    col_mine = lax.dynamic_slice_in_dim(col_scale, offset, mine_rows, 0)
    both = gather_directly(jnp.stack([row_scale, logz], axis=1), "batch", 0)
    pieces = lax.all_gather(
        jnp.concatenate((tn_group, sn_group), axis=1), "batch", axis=0, tiled=True
    )
    grad_protos = protos_grad(pieces, c_mine, col_mine, both.T, rows_all, scale)
    return (grad_student, grad_protos)


def solution(mesh):
    return jax.shard_map(
        per_device,
        mesh=mesh,
        in_specs=(P(("proto", "batch"), None), P(("proto", "batch"), None), P("proto", None)),
        out_specs=(P(("proto", "batch"), None), P(("proto", "batch"), None)),
        check_vma=False,
    )
```

```python
import math

import jax
import jax.numpy as jnp
from jax import lax
from jax.sharding import PartitionSpec as P
from jax.experimental import pallas as pl
from jax.experimental.pallas import tpu as pltpu
import functools

ITERS = 3


teacher_temp = 0.05
student_temp = 0.1

def _protos_kernel(ts_ref, c_ref, col_ref, al_ref, out_ref, *, rows_all, scale, width):
    @pl.when(pl.program_id(0) == 0)
    def _():
        out_ref[...] = jnp.zeros_like(out_ref)

    t = ts_ref[:, :width]
    s = ts_ref[:, width:]
    c = c_ref[...]
    dims = (((1,), (1,)), ((), ()))
    tl = lax.dot_general(c, t, dims, preferred_element_type=jnp.float32)
    sl = lax.dot_general(c, s, dims, preferred_element_type=jnp.float32)
    a = al_ref[0:1, :]
    logz = al_ref[1:2, :]
    target = rows_all * jnp.exp(tl / teacher_temp) * a * col_ref[...]
    probs = jnp.exp(sl / student_temp - logz)
    g = (scale * (probs - target)).astype(jnp.bfloat16)
    out_ref[...] += jnp.dot(g, s, preferred_element_type=jnp.float32)


def protos_grad(ts, c_mine, col_mine, al, rows_all, scale, block=2048, interpret=False):
    n, w2 = ts.shape
    width = w2 // 2
    m = c_mine.shape[0]
    kern = functools.partial(_protos_kernel, rows_all=rows_all, scale=scale, width=width)
    out = pl.pallas_call(
        kern,
        grid=(n // block,),
        in_specs=[
            pl.BlockSpec((block, w2), lambda i: (i, 0)),
            pl.BlockSpec((m, width), lambda i: (0, 0)),
            pl.BlockSpec((m, 1), lambda i: (0, 0)),
            pl.BlockSpec((2, block), lambda i: (0, i)),
        ],
        out_specs=pl.BlockSpec((m, width), lambda i: (0, 0)),
        out_shape=jax.ShapeDtypeStruct((m, width), jnp.float32),
        compiler_params=pltpu.CompilerParams(dimension_semantics=("arbitrary",)),
        interpret=interpret,
    )(ts, c_mine, col_mine.reshape(m, 1), al)
    return out / student_temp


def side_by_side(arrays, axis, dim, along):
    ends, at = ([], 0)
    for a in arrays[:-1]:
        at += a.shape[along]
        ends.append(at)
    both = jnp.concatenate(arrays, axis=along)
    return tuple(jnp.split(lax.all_gather(both, axis, axis=dim, tiled=True), ends, axis=along))


def cut_along(value, dim, length):
    lengths = value.shape
    parts = value.reshape(*lengths[:dim], length, lengths[dim] // length, *lengths[dim + 1 :])
    return jnp.moveaxis(parts, dim, 0)


def summed_on_arrival(value, axis, dim):
    parts = cut_along(value, dim, lax.axis_size(axis))
    arrived = lax.all_to_all(parts, axis, split_axis=0, concat_axis=0, tiled=True)
    return arrived.sum(axis=0)


def laid_out(parts, dim):
    parts = jnp.moveaxis(parts, 0, dim)
    lengths = parts.shape
    return parts.reshape(*lengths[:dim], lengths[dim] * lengths[dim + 1], *lengths[dim + 2 :])


def copy_for_each(value, axis):
    copies = jnp.broadcast_to(value, (lax.axis_size(axis), *value.shape))
    return lax.all_to_all(copies, axis, split_axis=0, concat_axis=0, tiled=True)


def gather_directly(value, axis, dim):
    return laid_out(copy_for_each(value, axis), dim)


def over_copies(value, axis):
    return copy_for_each(value, axis).sum(axis=0)


def gather_turned(arrays, axis, dims):
    turned = [jnp.moveaxis(a, dim, 0) for a, dim in zip(arrays, dims)]
    widths = [t[0].size for t in turned]
    both = jnp.concatenate([t.reshape(-1, w) for t, w in zip(turned, widths)], axis=1)
    out = lax.all_gather(both, axis, axis=0, tiled=True)
    parts = jnp.split(out, [sum(widths[:k]) for k in range(1, len(widths))], axis=1)
    return tuple(
        (
            jnp.moveaxis(b.reshape(-1, *t.shape[1:]), 0, dim)
            for b, t, dim in zip(parts, turned, dims)
        )
    )


def unit_rows(value):
    full = value.astype(jnp.float32)
    return (
        full
        * lax.rsqrt(jnp.mean(full * full, axis=1, keepdims=True) + 1e-06)
        / math.sqrt(value.shape[1])
    )


def against(left, right):
    return lax.dot_general(
        left, right, (((1,), (1,)), ((), ())), preferred_element_type=jnp.float32
    )


def per_device(teacher, student, prototypes):
    n_proto = lax.axis_size("proto")
    n_batch = lax.axis_size("batch")
    own_rows = teacher.shape[0]
    count_all = prototypes.shape[0] * n_proto
    rows_all = own_rows * n_proto * n_batch
    tn = unit_rows(teacher).astype(jnp.bfloat16)
    sn = unit_rows(student).astype(jnp.bfloat16)
    cn = unit_rows(prototypes).astype(jnp.bfloat16)
    tn_group, sn_group = side_by_side((tn, sn), "proto", 0, 1)
    weight = jnp.exp(against(tn_group, cn) / teacher_temp)
    row_scale = jnp.ones((tn_group.shape[0],), jnp.float32)
    col_scale = None
    for step in range(ITERS):
        mass_local = jnp.sum(weight * row_scale[:, None], axis=0)
        share = summed_on_arrival(mass_local, "batch", 0)
        col_scale = gather_directly(1.0 / (count_all * share), "batch", 0)
        sample_local = jnp.sum(weight * col_scale[None, :], axis=1)
        row_scale = 1.0 / (rows_all * over_copies(sample_local, "proto"))
    targets = rows_all * weight * row_scale[:, None] * col_scale[None, :]
    logits = against(sn_group, cn) / student_temp
    logz = jnp.log(over_copies(jnp.sum(jnp.exp(logits), axis=1), "proto"))
    logp = logits - logz[:, None]
    scale = 16.0 * math.sqrt(count_all)
    grads = (scale * (jnp.exp(logp) - targets)).astype(jnp.bfloat16)
    sn_partial = jnp.dot(grads, cn, preferred_element_type=jnp.float32) / student_temp
    mine_rows = prototypes.shape[0] // n_batch
    offset = lax.axis_index("batch") * mine_rows
    c_mine = lax.dynamic_slice_in_dim(cn, offset, mine_rows, 0)
    col_mine = lax.dynamic_slice_in_dim(col_scale, offset, mine_rows, 0)
    both = gather_directly(jnp.stack([row_scale, logz], axis=1), "batch", 0)
    sn_partial, both = lax.optimization_barrier((sn_partial, both))
    grad_sn = summed_on_arrival(sn_partial, "proto", 0)
    pieces = lax.all_gather(
        jnp.concatenate((tn_group, sn_group), axis=1), "batch", axis=0, tiled=True
    )
    grad_protos = protos_grad(pieces, c_mine, col_mine, both.T, rows_all, scale)
    _, pull = jax.vjp(unit_rows, student.astype(jnp.float32))
    grad_student = pull(grad_sn)[0]
    return (grad_student, grad_protos)


def solution(mesh):
    return jax.shard_map(
        per_device,
        mesh=mesh,
        in_specs=(P(("proto", "batch"), None), P(("proto", "batch"), None), P("proto", None)),
        out_specs=(P(("proto", "batch"), None), P(("proto", "batch"), None)),
        check_vma=False,
    )
```

```python
import math

import jax
import jax.numpy as jnp
from jax import lax
from jax.sharding import PartitionSpec as P
from jax.experimental import pallas as pl
from jax.experimental.pallas import tpu as pltpu
import functools

ITERS = 3


teacher_temp = 0.05
student_temp = 0.1

def _protos_kernel(ts_ref, c_ref, col_ref, al_ref, out_ref, *, width):
    @pl.when(pl.program_id(0) == 0)
    def _():
        out_ref[...] = jnp.zeros_like(out_ref)

    t = ts_ref[:, :width]
    s = ts_ref[:, width:]
    c = c_ref[...]
    dims = (((1,), (1,)), ((), ()))
    tl = lax.dot_general(c, t, dims, preferred_element_type=jnp.float32)
    sl = lax.dot_general(c, s, dims, preferred_element_type=jnp.float32)
    fac = al_ref[0:1, :]
    shift = al_ref[1:2, :]
    target = jnp.exp(tl * (1.0 / teacher_temp)) * fac * col_ref[...]
    probs = jnp.exp(sl * (1.0 / student_temp) - shift)
    g = (probs - target).astype(jnp.bfloat16)
    out_ref[...] += jnp.dot(g, s, preferred_element_type=jnp.float32)


def protos_grad(ts, c_mine, col_mine, scales, rows_all, scale, block=2048, interpret=False):
    n, w2 = ts.shape
    width = w2 // 2
    m = c_mine.shape[0]
    al = jnp.stack([(scale * rows_all) * scales[:, 0], scales[:, 1] - math.log(scale)])
    out = pl.pallas_call(
        functools.partial(_protos_kernel, width=width),
        grid=(n // block,),
        in_specs=[
            pl.BlockSpec((block, w2), lambda i: (i, 0)),
            pl.BlockSpec((m, width), lambda i: (0, 0)),
            pl.BlockSpec((m, 1), lambda i: (0, 0)),
            pl.BlockSpec((2, block), lambda i: (0, i)),
        ],
        out_specs=pl.BlockSpec((m, width), lambda i: (0, 0)),
        out_shape=jax.ShapeDtypeStruct((m, width), jnp.float32),
        compiler_params=pltpu.CompilerParams(dimension_semantics=("arbitrary",)),
        interpret=interpret,
    )(ts, c_mine, col_mine.reshape(m, 1), al)
    return out / student_temp


def side_by_side(arrays, axis, dim, along):
    ends, at = ([], 0)
    for a in arrays[:-1]:
        at += a.shape[along]
        ends.append(at)
    both = jnp.concatenate(arrays, axis=along)
    return tuple(jnp.split(lax.all_gather(both, axis, axis=dim, tiled=True), ends, axis=along))


def cut_along(value, dim, length):
    lengths = value.shape
    parts = value.reshape(*lengths[:dim], length, lengths[dim] // length, *lengths[dim + 1 :])
    return jnp.moveaxis(parts, dim, 0)


def summed_on_arrival(value, axis, dim):
    parts = cut_along(value, dim, lax.axis_size(axis))
    arrived = lax.all_to_all(parts, axis, split_axis=0, concat_axis=0, tiled=True)
    return arrived.sum(axis=0)


def laid_out(parts, dim):
    parts = jnp.moveaxis(parts, 0, dim)
    lengths = parts.shape
    return parts.reshape(*lengths[:dim], lengths[dim] * lengths[dim + 1], *lengths[dim + 2 :])


def copy_for_each(value, axis):
    copies = jnp.broadcast_to(value, (lax.axis_size(axis), *value.shape))
    return lax.all_to_all(copies, axis, split_axis=0, concat_axis=0, tiled=True)


def gather_directly(value, axis, dim):
    return laid_out(copy_for_each(value, axis), dim)


def over_copies(value, axis):
    return copy_for_each(value, axis).sum(axis=0)


def gather_turned(arrays, axis, dims):
    turned = [jnp.moveaxis(a, dim, 0) for a, dim in zip(arrays, dims)]
    widths = [t[0].size for t in turned]
    both = jnp.concatenate([t.reshape(-1, w) for t, w in zip(turned, widths)], axis=1)
    out = lax.all_gather(both, axis, axis=0, tiled=True)
    parts = jnp.split(out, [sum(widths[:k]) for k in range(1, len(widths))], axis=1)
    return tuple(
        (
            jnp.moveaxis(b.reshape(-1, *t.shape[1:]), 0, dim)
            for b, t, dim in zip(parts, turned, dims)
        )
    )


def unit_rows(value):
    full = value.astype(jnp.float32)
    return (
        full
        * lax.rsqrt(jnp.mean(full * full, axis=1, keepdims=True) + 1e-06)
        / math.sqrt(value.shape[1])
    )


def against(left, right):
    return lax.dot_general(
        left, right, (((1,), (1,)), ((), ())), preferred_element_type=jnp.float32
    )


def per_device(teacher, student, prototypes):
    n_proto = lax.axis_size("proto")
    n_batch = lax.axis_size("batch")
    own_rows = teacher.shape[0]
    count_all = prototypes.shape[0] * n_proto
    rows_all = own_rows * n_proto * n_batch
    tn = unit_rows(teacher).astype(jnp.bfloat16)
    sn = unit_rows(student).astype(jnp.bfloat16)
    cn = unit_rows(prototypes).astype(jnp.bfloat16)
    tn_group, sn_group = side_by_side((tn, sn), "proto", 0, 1)
    weight = jnp.exp(against(tn_group, cn) / teacher_temp)
    row_scale = jnp.ones((tn_group.shape[0],), jnp.float32)
    col_scale = None
    for step in range(ITERS):
        mass_local = jnp.sum(weight * row_scale[:, None], axis=0)
        share = summed_on_arrival(mass_local, "batch", 0)
        col_scale = gather_directly(1.0 / (count_all * share), "batch", 0)
        sample_local = jnp.sum(weight * col_scale[None, :], axis=1)
        row_scale = 1.0 / (rows_all * over_copies(sample_local, "proto"))
    targets = rows_all * weight * row_scale[:, None] * col_scale[None, :]
    logits = against(sn_group, cn) / student_temp
    logz = jnp.log(over_copies(jnp.sum(jnp.exp(logits), axis=1), "proto"))
    logp = logits - logz[:, None]
    scale = 16.0 * math.sqrt(count_all)
    grads = (scale * (jnp.exp(logp) - targets)).astype(jnp.bfloat16)
    sn_partial = jnp.dot(grads, cn, preferred_element_type=jnp.float32) / student_temp
    mine_rows = prototypes.shape[0] // n_batch
    offset = lax.axis_index("batch") * mine_rows
    c_mine = lax.dynamic_slice_in_dim(cn, offset, mine_rows, 0)
    col_mine = lax.dynamic_slice_in_dim(col_scale, offset, mine_rows, 0)
    both = gather_directly(jnp.stack([row_scale, logz], axis=1), "batch", 0)
    sn_partial, both = lax.optimization_barrier((sn_partial, both))
    grad_sn = summed_on_arrival(sn_partial, "proto", 0)
    pieces = lax.all_gather(
        jnp.concatenate((tn_group, sn_group), axis=1), "batch", axis=0, tiled=True
    )
    grad_protos = protos_grad(pieces, c_mine, col_mine, both, rows_all, scale)
    _, pull = jax.vjp(unit_rows, student.astype(jnp.float32))
    grad_student = pull(grad_sn)[0]
    return (grad_student, grad_protos)


def solution(mesh):
    return jax.shard_map(
        per_device,
        mesh=mesh,
        in_specs=(P(("proto", "batch"), None), P(("proto", "batch"), None), P("proto", None)),
        out_specs=(P(("proto", "batch"), None), P(("proto", "batch"), None)),
        check_vma=False,
    )
```

```python
import math

import jax
import jax.numpy as jnp
from jax import lax
from jax.sharding import PartitionSpec as P
from jax.experimental import pallas as pl
from jax.experimental.pallas import tpu as pltpu
import functools

ITERS = 3


teacher_temp = 0.05
student_temp = 0.1

def _protos_kernel(ts_ref, c_ref, col_ref, al_ref, out_ref, *, rows_all, scale, width):
    @pl.when(pl.program_id(0) == 0)
    def _():
        out_ref[...] = jnp.zeros_like(out_ref)

    t = ts_ref[:, :width]
    s = ts_ref[:, width:]
    c = c_ref[...]
    dims = (((1,), (1,)), ((), ()))
    tl = lax.dot_general(c, t, dims, preferred_element_type=jnp.float32)
    sl = lax.dot_general(c, s, dims, preferred_element_type=jnp.float32)
    a = al_ref[0:1, :]
    logz = al_ref[1:2, :]
    target = rows_all * jnp.exp(tl / teacher_temp) * a * col_ref[...]
    probs = jnp.exp(sl / student_temp - logz)
    g = (scale * (probs - target)).astype(jnp.bfloat16)
    out_ref[...] += jnp.dot(g, s, preferred_element_type=jnp.float32)


def protos_grad(ts, c_mine, col_mine, al, rows_all, scale, block=4096, interpret=False):
    n, w2 = ts.shape
    width = w2 // 2
    m = c_mine.shape[0]
    kern = functools.partial(_protos_kernel, rows_all=rows_all, scale=scale, width=width)
    out = pl.pallas_call(
        kern,
        grid=(n // block,),
        in_specs=[
            pl.BlockSpec((block, w2), lambda i: (i, 0)),
            pl.BlockSpec((m, width), lambda i: (0, 0)),
            pl.BlockSpec((m, 1), lambda i: (0, 0)),
            pl.BlockSpec((2, block), lambda i: (0, i)),
        ],
        out_specs=pl.BlockSpec((m, width), lambda i: (0, 0)),
        out_shape=jax.ShapeDtypeStruct((m, width), jnp.float32),
        compiler_params=pltpu.CompilerParams(dimension_semantics=("arbitrary",)),
        interpret=interpret,
    )(ts, c_mine, col_mine.reshape(m, 1), al)
    return out / student_temp


def side_by_side(arrays, axis, dim, along):
    ends, at = ([], 0)
    for a in arrays[:-1]:
        at += a.shape[along]
        ends.append(at)
    both = jnp.concatenate(arrays, axis=along)
    return tuple(jnp.split(lax.all_gather(both, axis, axis=dim, tiled=True), ends, axis=along))


def cut_along(value, dim, length):
    lengths = value.shape
    parts = value.reshape(*lengths[:dim], length, lengths[dim] // length, *lengths[dim + 1 :])
    return jnp.moveaxis(parts, dim, 0)


def summed_on_arrival(value, axis, dim):
    parts = cut_along(value, dim, lax.axis_size(axis))
    arrived = lax.all_to_all(parts, axis, split_axis=0, concat_axis=0, tiled=True)
    return arrived.sum(axis=0)


def laid_out(parts, dim):
    parts = jnp.moveaxis(parts, 0, dim)
    lengths = parts.shape
    return parts.reshape(*lengths[:dim], lengths[dim] * lengths[dim + 1], *lengths[dim + 2 :])


def copy_for_each(value, axis):
    copies = jnp.broadcast_to(value, (lax.axis_size(axis), *value.shape))
    return lax.all_to_all(copies, axis, split_axis=0, concat_axis=0, tiled=True)


def gather_directly(value, axis, dim):
    return laid_out(copy_for_each(value, axis), dim)


def over_copies(value, axis):
    return copy_for_each(value, axis).sum(axis=0)


def gather_turned(arrays, axis, dims):
    turned = [jnp.moveaxis(a, dim, 0) for a, dim in zip(arrays, dims)]
    widths = [t[0].size for t in turned]
    both = jnp.concatenate([t.reshape(-1, w) for t, w in zip(turned, widths)], axis=1)
    out = lax.all_gather(both, axis, axis=0, tiled=True)
    parts = jnp.split(out, [sum(widths[:k]) for k in range(1, len(widths))], axis=1)
    return tuple(
        (
            jnp.moveaxis(b.reshape(-1, *t.shape[1:]), 0, dim)
            for b, t, dim in zip(parts, turned, dims)
        )
    )


def unit_rows(value):
    full = value.astype(jnp.float32)
    return (
        full
        * lax.rsqrt(jnp.mean(full * full, axis=1, keepdims=True) + 1e-06)
        / math.sqrt(value.shape[1])
    )


def against(left, right):
    return lax.dot_general(
        left, right, (((1,), (1,)), ((), ())), preferred_element_type=jnp.float32
    )


def per_device(teacher, student, prototypes):
    n_proto = lax.axis_size("proto")
    n_batch = lax.axis_size("batch")
    own_rows = teacher.shape[0]
    count_all = prototypes.shape[0] * n_proto
    rows_all = own_rows * n_proto * n_batch
    tn = unit_rows(teacher).astype(jnp.bfloat16)
    sn = unit_rows(student).astype(jnp.bfloat16)
    cn = unit_rows(prototypes).astype(jnp.bfloat16)
    width = tn.shape[1]
    group = gather_directly(jnp.concatenate((tn, sn), axis=1), "proto", 0)
    tn_group, sn_group = group[:, :width], group[:, width:]
    weight = jnp.exp(against(tn_group, cn) / teacher_temp)
    row_scale = jnp.ones((tn_group.shape[0],), jnp.float32)
    col_scale = None
    for step in range(ITERS):
        mass_local = jnp.sum(weight * row_scale[:, None], axis=0)
        share = summed_on_arrival(mass_local, "batch", 0)
        col_scale = gather_directly(1.0 / (count_all * share), "batch", 0)
        sample_local = jnp.sum(weight * col_scale[None, :], axis=1)
        row_scale = 1.0 / (rows_all * over_copies(sample_local, "proto"))
    targets = rows_all * weight * row_scale[:, None] * col_scale[None, :]
    logits = against(sn_group, cn) / student_temp
    logz = jnp.log(over_copies(jnp.sum(jnp.exp(logits), axis=1), "proto"))
    logp = logits - logz[:, None]
    scale = 16.0 * math.sqrt(count_all)
    grads = (scale * (jnp.exp(logp) - targets)).astype(jnp.bfloat16)
    sn_partial = jnp.dot(grads, cn, preferred_element_type=jnp.float32) / student_temp
    mine_rows = prototypes.shape[0] // n_batch
    offset = lax.axis_index("batch") * mine_rows
    c_mine = lax.dynamic_slice_in_dim(cn, offset, mine_rows, 0)
    col_mine = lax.dynamic_slice_in_dim(col_scale, offset, mine_rows, 0)
    both = gather_directly(jnp.stack([row_scale, logz], axis=1), "batch", 0)
    sn_partial, both = lax.optimization_barrier((sn_partial, both))
    grad_sn = summed_on_arrival(sn_partial, "proto", 0)
    pieces = lax.all_gather(
        jnp.concatenate((tn_group, sn_group), axis=1), "batch", axis=0, tiled=True
    )
    grad_protos = protos_grad(pieces, c_mine, col_mine, both.T, rows_all, scale)
    _, pull = jax.vjp(unit_rows, student.astype(jnp.float32))
    grad_student = pull(grad_sn)[0]
    return (grad_student, grad_protos)


def solution(mesh):
    return jax.shard_map(
        per_device,
        mesh=mesh,
        in_specs=(P(("proto", "batch"), None), P(("proto", "batch"), None), P("proto", None)),
        out_specs=(P(("proto", "batch"), None), P(("proto", "batch"), None)),
        check_vma=False,
    )
```

```python
import math

import jax
import jax.numpy as jnp
from jax import lax
from jax.sharding import PartitionSpec as P
from jax.experimental import pallas as pl
from jax.experimental.pallas import tpu as pltpu
import functools

ITERS = 3


teacher_temp = 0.05
student_temp = 0.1

def _protos_kernel(ts_ref, c_ref, col_ref, al_ref, out_ref, *, rows_all, scale, width):
    @pl.when(pl.program_id(0) == 0)
    def _():
        out_ref[...] = jnp.zeros_like(out_ref)

    t = ts_ref[:, :width]
    s = ts_ref[:, width:]
    c = c_ref[...]
    dims = (((1,), (1,)), ((), ()))
    tl = lax.dot_general(c, t, dims, preferred_element_type=jnp.float32)
    sl = lax.dot_general(c, s, dims, preferred_element_type=jnp.float32)
    a = al_ref[0:1, :]
    logz = al_ref[1:2, :]
    target = rows_all * jnp.exp(tl / teacher_temp) * a * col_ref[...]
    probs = jnp.exp(sl / student_temp - logz)
    g = (scale * (probs - target)).astype(jnp.bfloat16)
    out_ref[...] += jnp.dot(g, s, preferred_element_type=jnp.float32)


def _col_kernel(t_ref, c_ref, a_ref, out_ref):
    dims = (((1,), (1,)), ((), ()))
    w = jnp.exp(
        lax.dot_general(t_ref[...], c_ref[...], dims, preferred_element_type=jnp.float32)
        / teacher_temp
    )
    out_ref[...] = jnp.sum(w * a_ref[...], axis=0, keepdims=True)


def _row_kernel(t_ref, c_ref, col_ref, out_ref):
    @pl.when(pl.program_id(0) == 0)
    def _():
        out_ref[...] = jnp.zeros_like(out_ref)

    dims = (((1,), (1,)), ((), ()))
    w = jnp.exp(
        lax.dot_general(t_ref[...], c_ref[...], dims, preferred_element_type=jnp.float32)
        / teacher_temp
    )
    out_ref[...] += jnp.sum(w * col_ref[...], axis=1, keepdims=True)


def sweep(tn_group, cn, vec, by_column, block=2048):
    rows, width = tn_group.shape
    count = cn.shape[0]
    specs = [
        pl.BlockSpec((rows, width), lambda j: (0, 0)),
        pl.BlockSpec((block, width), lambda j: (j, 0)),
    ]
    if by_column:
        kern, vec = _col_kernel, vec.reshape(rows, 1)
        specs.append(pl.BlockSpec((rows, 1), lambda j: (0, 0)))
        out_spec = pl.BlockSpec((1, block), lambda j: (0, j))
        out_shape = jax.ShapeDtypeStruct((1, count), jnp.float32)
    else:
        kern, vec = _row_kernel, vec.reshape(1, count)
        specs.append(pl.BlockSpec((1, block), lambda j: (0, j)))
        out_spec = pl.BlockSpec((rows, 1), lambda j: (0, 0))
        out_shape = jax.ShapeDtypeStruct((rows, 1), jnp.float32)
    out = pl.pallas_call(
        kern,
        grid=(count // block,),
        in_specs=specs,
        out_specs=out_spec,
        out_shape=out_shape,
        compiler_params=pltpu.CompilerParams(dimension_semantics=("arbitrary",)),
        cost_estimate=pl.CostEstimate(
            flops=2 * rows * count * width,
            transcendentals=rows * count,
            bytes_accessed=2 * (rows + count) * width,
        ),
    )(tn_group, cn, vec)
    return out.reshape(-1)


def protos_grad(ts, c_mine, col_mine, al, rows_all, scale, block=8192, interpret=False):
    n, w2 = ts.shape
    width = w2 // 2
    m = c_mine.shape[0]
    kern = functools.partial(_protos_kernel, rows_all=rows_all, scale=scale, width=width)
    out = pl.pallas_call(
        kern,
        grid=(n // block,),
        in_specs=[
            pl.BlockSpec((block, w2), lambda i: (i, 0)),
            pl.BlockSpec((m, width), lambda i: (0, 0)),
            pl.BlockSpec((m, 1), lambda i: (0, 0)),
            pl.BlockSpec((2, block), lambda i: (0, i)),
        ],
        out_specs=pl.BlockSpec((m, width), lambda i: (0, 0)),
        out_shape=jax.ShapeDtypeStruct((m, width), jnp.float32),
        compiler_params=pltpu.CompilerParams(
            dimension_semantics=("arbitrary",), vmem_limit_bytes=56 * 1024 * 1024
        ),
        cost_estimate=pl.CostEstimate(
            flops=6 * n * m * width,
            transcendentals=2 * n * m,
            bytes_accessed=2 * n * w2 + 4 * m * width,
        ),
        interpret=interpret,
    )(ts, c_mine, col_mine.reshape(m, 1), al)
    return out / student_temp


def side_by_side(arrays, axis, dim, along):
    ends, at = ([], 0)
    for a in arrays[:-1]:
        at += a.shape[along]
        ends.append(at)
    both = jnp.concatenate(arrays, axis=along)
    return tuple(jnp.split(lax.all_gather(both, axis, axis=dim, tiled=True), ends, axis=along))


def cut_along(value, dim, length):
    lengths = value.shape
    parts = value.reshape(*lengths[:dim], length, lengths[dim] // length, *lengths[dim + 1 :])
    return jnp.moveaxis(parts, dim, 0)


def summed_on_arrival(value, axis, dim):
    parts = cut_along(value, dim, lax.axis_size(axis))
    arrived = lax.all_to_all(parts, axis, split_axis=0, concat_axis=0, tiled=True)
    return arrived.sum(axis=0)


def laid_out(parts, dim):
    parts = jnp.moveaxis(parts, 0, dim)
    lengths = parts.shape
    return parts.reshape(*lengths[:dim], lengths[dim] * lengths[dim + 1], *lengths[dim + 2 :])


def copy_for_each(value, axis):
    copies = jnp.broadcast_to(value, (lax.axis_size(axis), *value.shape))
    return lax.all_to_all(copies, axis, split_axis=0, concat_axis=0, tiled=True)


def gather_directly(value, axis, dim):
    return laid_out(copy_for_each(value, axis), dim)


def over_copies(value, axis):
    return copy_for_each(value, axis).sum(axis=0)


def gather_turned(arrays, axis, dims):
    turned = [jnp.moveaxis(a, dim, 0) for a, dim in zip(arrays, dims)]
    widths = [t[0].size for t in turned]
    both = jnp.concatenate([t.reshape(-1, w) for t, w in zip(turned, widths)], axis=1)
    out = lax.all_gather(both, axis, axis=0, tiled=True)
    parts = jnp.split(out, [sum(widths[:k]) for k in range(1, len(widths))], axis=1)
    return tuple(
        (
            jnp.moveaxis(b.reshape(-1, *t.shape[1:]), 0, dim)
            for b, t, dim in zip(parts, turned, dims)
        )
    )


def unit_rows(value):
    full = value.astype(jnp.float32)
    return (
        full
        * lax.rsqrt(jnp.mean(full * full, axis=1, keepdims=True) + 1e-06)
        / math.sqrt(value.shape[1])
    )


def against(left, right):
    return lax.dot_general(
        left, right, (((1,), (1,)), ((), ())), preferred_element_type=jnp.float32
    )


def per_device(teacher, student, prototypes):
    n_proto = lax.axis_size("proto")
    n_batch = lax.axis_size("batch")
    own_rows = teacher.shape[0]
    count_all = prototypes.shape[0] * n_proto
    rows_all = own_rows * n_proto * n_batch
    tn = unit_rows(teacher).astype(jnp.bfloat16)
    sn = unit_rows(student).astype(jnp.bfloat16)
    cn = unit_rows(prototypes).astype(jnp.bfloat16)
    width = tn.shape[1]
    group = gather_directly(jnp.concatenate((tn, sn), axis=1), "proto", 0)
    tn_group, sn_group = group[:, :width], group[:, width:]
    weight = jnp.exp(against(tn_group, cn) / teacher_temp)
    row_scale = jnp.ones((tn_group.shape[0],), jnp.float32)
    col_scale = None
    for step in range(ITERS):
        if step == 0:
            mass_local = jnp.sum(weight * row_scale[:, None], axis=0)
        else:
            mass_local = sweep(tn_group, cn, row_scale, True)
        share = summed_on_arrival(mass_local, "batch", 0)
        col_scale = gather_directly(1.0 / (count_all * share), "batch", 0)
        sample_local = sweep(tn_group, cn, col_scale, False)
        row_scale = 1.0 / (rows_all * over_copies(sample_local, "proto"))
    targets = rows_all * weight * row_scale[:, None] * col_scale[None, :]
    logits = against(sn_group, cn) / student_temp
    logz = jnp.log(over_copies(jnp.sum(jnp.exp(logits), axis=1), "proto"))
    logp = logits - logz[:, None]
    scale = 16.0 * math.sqrt(count_all)
    grads = (scale * (jnp.exp(logp) - targets)).astype(jnp.bfloat16)
    sn_partial = jnp.dot(grads, cn, preferred_element_type=jnp.float32) / student_temp
    mine_rows = prototypes.shape[0] // n_batch
    offset = lax.axis_index("batch") * mine_rows
    c_mine = lax.dynamic_slice_in_dim(cn, offset, mine_rows, 0)
    col_mine = lax.dynamic_slice_in_dim(col_scale, offset, mine_rows, 0)
    both = gather_directly(jnp.stack([row_scale, logz], axis=1), "batch", 0)
    sn_partial, both = lax.optimization_barrier((sn_partial, both))
    grad_sn = summed_on_arrival(sn_partial, "proto", 0)
    pieces = lax.all_gather(
        jnp.concatenate((tn_group, sn_group), axis=1), "batch", axis=0, tiled=True
    )
    grad_protos = protos_grad(pieces, c_mine, col_mine, both.T, rows_all, scale)
    _, pull = jax.vjp(unit_rows, student.astype(jnp.float32))
    grad_student = pull(grad_sn)[0]
    return (grad_student, grad_protos)


def solution(mesh):
    return jax.shard_map(
        per_device,
        mesh=mesh,
        in_specs=(P(("proto", "batch"), None), P(("proto", "batch"), None), P("proto", None)),
        out_specs=(P(("proto", "batch"), None), P(("proto", "batch"), None)),
        check_vma=False,
    )
```

```python
import math

import jax
import jax.numpy as jnp
from jax import lax
from jax.sharding import PartitionSpec as P
from jax.experimental import pallas as pl
from jax.experimental.pallas import tpu as pltpu
import functools

ITERS = 3


teacher_temp = 0.05
student_temp = 0.1

def _protos_kernel(ts_ref, c_ref, col_ref, al_ref, out_ref, *, rows_all, scale, width):
    @pl.when(pl.program_id(0) == 0)
    def _():
        out_ref[...] = jnp.zeros_like(out_ref)

    t = ts_ref[:, :width]
    s = ts_ref[:, width:]
    c = c_ref[...]
    dims = (((1,), (1,)), ((), ()))
    tl = lax.dot_general(c, t, dims, preferred_element_type=jnp.float32)
    sl = lax.dot_general(c, s, dims, preferred_element_type=jnp.float32)
    a = al_ref[0:1, :]
    logz = al_ref[1:2, :]
    target = rows_all * jnp.exp(tl / teacher_temp) * a * col_ref[...]
    probs = jnp.exp(sl / student_temp - logz)
    g = (scale * (probs - target)).astype(jnp.bfloat16)
    out_ref[...] += jnp.dot(g, s, preferred_element_type=jnp.float32)


def _col_kernel(t_ref, c_ref, a_ref, out_ref):
    dims = (((1,), (1,)), ((), ()))
    w = jnp.exp(
        lax.dot_general(t_ref[...], c_ref[...], dims, preferred_element_type=jnp.float32)
        / teacher_temp
    )
    out_ref[...] = jnp.sum(w * a_ref[...], axis=0, keepdims=True)


def _row_kernel(t_ref, c_ref, col_ref, out_ref):
    @pl.when(pl.program_id(0) == 0)
    def _():
        out_ref[...] = jnp.zeros_like(out_ref)

    dims = (((1,), (1,)), ((), ()))
    w = jnp.exp(
        lax.dot_general(t_ref[...], c_ref[...], dims, preferred_element_type=jnp.float32)
        / teacher_temp
    )
    out_ref[...] += jnp.sum(w * col_ref[...], axis=1, keepdims=True)


def sweep(tn_group, cn, vec, by_column, block=2048):
    rows, width = tn_group.shape
    count = cn.shape[0]
    specs = [
        pl.BlockSpec((rows, width), lambda j: (0, 0)),
        pl.BlockSpec((block, width), lambda j: (j, 0)),
    ]
    if by_column:
        kern, vec = _col_kernel, vec.reshape(rows, 1)
        specs.append(pl.BlockSpec((rows, 1), lambda j: (0, 0)))
        out_spec = pl.BlockSpec((1, block), lambda j: (0, j))
        out_shape = jax.ShapeDtypeStruct((1, count), jnp.float32)
    else:
        kern, vec = _row_kernel, vec.reshape(1, count)
        specs.append(pl.BlockSpec((1, block), lambda j: (0, j)))
        out_spec = pl.BlockSpec((rows, 1), lambda j: (0, 0))
        out_shape = jax.ShapeDtypeStruct((rows, 1), jnp.float32)
    out = pl.pallas_call(
        kern,
        grid=(count // block,),
        in_specs=specs,
        out_specs=out_spec,
        out_shape=out_shape,
        compiler_params=pltpu.CompilerParams(
            dimension_semantics=("arbitrary",), vmem_limit_bytes=56 * 1024 * 1024
        ),
        cost_estimate=pl.CostEstimate(
            flops=2 * rows * count * width,
            transcendentals=rows * count,
            bytes_accessed=2 * (rows + count) * width,
        ),
    )(tn_group, cn, vec)
    return out.reshape(-1)


def protos_grad(ts, c_mine, col_mine, al, rows_all, scale, block=8192, interpret=False):
    n, w2 = ts.shape
    width = w2 // 2
    m = c_mine.shape[0]
    kern = functools.partial(_protos_kernel, rows_all=rows_all, scale=scale, width=width)
    out = pl.pallas_call(
        kern,
        grid=(n // block,),
        in_specs=[
            pl.BlockSpec((block, w2), lambda i: (i, 0)),
            pl.BlockSpec((m, width), lambda i: (0, 0)),
            pl.BlockSpec((m, 1), lambda i: (0, 0)),
            pl.BlockSpec((2, block), lambda i: (0, i)),
        ],
        out_specs=pl.BlockSpec((m, width), lambda i: (0, 0)),
        out_shape=jax.ShapeDtypeStruct((m, width), jnp.float32),
        compiler_params=pltpu.CompilerParams(
            dimension_semantics=("arbitrary",), vmem_limit_bytes=56 * 1024 * 1024
        ),
        cost_estimate=pl.CostEstimate(
            flops=6 * n * m * width,
            transcendentals=2 * n * m,
            bytes_accessed=2 * n * w2 + 4 * m * width,
        ),
        interpret=interpret,
    )(ts, c_mine, col_mine.reshape(m, 1), al)
    return out / student_temp


def side_by_side(arrays, axis, dim, along):
    ends, at = ([], 0)
    for a in arrays[:-1]:
        at += a.shape[along]
        ends.append(at)
    both = jnp.concatenate(arrays, axis=along)
    return tuple(jnp.split(lax.all_gather(both, axis, axis=dim, tiled=True), ends, axis=along))


def cut_along(value, dim, length):
    lengths = value.shape
    parts = value.reshape(*lengths[:dim], length, lengths[dim] // length, *lengths[dim + 1 :])
    return jnp.moveaxis(parts, dim, 0)


def summed_on_arrival(value, axis, dim):
    parts = cut_along(value, dim, lax.axis_size(axis))
    arrived = lax.all_to_all(parts, axis, split_axis=0, concat_axis=0, tiled=True)
    return arrived.sum(axis=0)


def laid_out(parts, dim):
    parts = jnp.moveaxis(parts, 0, dim)
    lengths = parts.shape
    return parts.reshape(*lengths[:dim], lengths[dim] * lengths[dim + 1], *lengths[dim + 2 :])


def copy_for_each(value, axis):
    copies = jnp.broadcast_to(value, (lax.axis_size(axis), *value.shape))
    return lax.all_to_all(copies, axis, split_axis=0, concat_axis=0, tiled=True)


def gather_directly(value, axis, dim):
    return laid_out(copy_for_each(value, axis), dim)


def over_copies(value, axis):
    return copy_for_each(value, axis).sum(axis=0)


def gather_turned(arrays, axis, dims):
    turned = [jnp.moveaxis(a, dim, 0) for a, dim in zip(arrays, dims)]
    widths = [t[0].size for t in turned]
    both = jnp.concatenate([t.reshape(-1, w) for t, w in zip(turned, widths)], axis=1)
    out = lax.all_gather(both, axis, axis=0, tiled=True)
    parts = jnp.split(out, [sum(widths[:k]) for k in range(1, len(widths))], axis=1)
    return tuple(
        (
            jnp.moveaxis(b.reshape(-1, *t.shape[1:]), 0, dim)
            for b, t, dim in zip(parts, turned, dims)
        )
    )


def unit_rows(value):
    full = value.astype(jnp.float32)
    return (
        full
        * lax.rsqrt(jnp.mean(full * full, axis=1, keepdims=True) + 1e-06)
        / math.sqrt(value.shape[1])
    )


def against(left, right):
    return lax.dot_general(
        left, right, (((1,), (1,)), ((), ())), preferred_element_type=jnp.float32
    )


def per_device(teacher, student, prototypes):
    n_proto = lax.axis_size("proto")
    n_batch = lax.axis_size("batch")
    own_rows = teacher.shape[0]
    count_all = prototypes.shape[0] * n_proto
    rows_all = own_rows * n_proto * n_batch
    tn = unit_rows(teacher).astype(jnp.bfloat16)
    sn = unit_rows(student).astype(jnp.bfloat16)
    cn = unit_rows(prototypes).astype(jnp.bfloat16)
    width = tn.shape[1]
    group = gather_directly(jnp.concatenate((tn, sn), axis=1), "proto", 0)
    tn_group, sn_group = group[:, :width], group[:, width:]
    weight = jnp.exp(against(tn_group, cn) / teacher_temp)
    row_scale = jnp.ones((tn_group.shape[0],), jnp.float32)
    col_scale = None
    for step in range(ITERS):
        mass_local = sweep(tn_group, cn, row_scale, True)
        share = summed_on_arrival(mass_local, "batch", 0)
        col_scale = gather_directly(1.0 / (count_all * share), "batch", 0)
        sample_local = sweep(tn_group, cn, col_scale, False)
        row_scale = 1.0 / (rows_all * over_copies(sample_local, "proto"))
    targets = rows_all * weight * row_scale[:, None] * col_scale[None, :]
    logits = against(sn_group, cn) / student_temp
    logz = jnp.log(over_copies(jnp.sum(jnp.exp(logits), axis=1), "proto"))
    logp = logits - logz[:, None]
    scale = 16.0 * math.sqrt(count_all)
    grads = (scale * (jnp.exp(logp) - targets)).astype(jnp.bfloat16)
    sn_partial = jnp.dot(grads, cn, preferred_element_type=jnp.float32) / student_temp
    mine_rows = prototypes.shape[0] // n_batch
    offset = lax.axis_index("batch") * mine_rows
    c_mine = lax.dynamic_slice_in_dim(cn, offset, mine_rows, 0)
    col_mine = lax.dynamic_slice_in_dim(col_scale, offset, mine_rows, 0)
    both = gather_directly(jnp.stack([row_scale, logz], axis=1), "batch", 0)
    sn_partial, both = lax.optimization_barrier((sn_partial, both))
    grad_sn = summed_on_arrival(sn_partial, "proto", 0)
    pieces = lax.all_gather(
        jnp.concatenate((tn_group, sn_group), axis=1), "batch", axis=0, tiled=True
    )
    grad_protos = protos_grad(pieces, c_mine, col_mine, both.T, rows_all, scale)
    _, pull = jax.vjp(unit_rows, student.astype(jnp.float32))
    grad_student = pull(grad_sn)[0]
    return (grad_student, grad_protos)


def solution(mesh):
    return jax.shard_map(
        per_device,
        mesh=mesh,
        in_specs=(P(("proto", "batch"), None), P(("proto", "batch"), None), P("proto", None)),
        out_specs=(P(("proto", "batch"), None), P(("proto", "batch"), None)),
        check_vma=False,
    )
```

```python
import math

import jax
import jax.numpy as jnp
from jax import lax
from jax.sharding import PartitionSpec as P
from jax.experimental import pallas as pl
from jax.experimental.pallas import tpu as pltpu
import functools

ITERS = 3


teacher_temp = 0.05
student_temp = 0.1

def _protos_kernel(ts_ref, c_ref, col_ref, al_ref, out_ref, *, rows_all, scale, width):
    @pl.when(pl.program_id(0) == 0)
    def _():
        out_ref[...] = jnp.zeros_like(out_ref)

    t = ts_ref[:, :width]
    s = ts_ref[:, width:]
    c = c_ref[...]
    dims = (((1,), (1,)), ((), ()))
    tl = lax.dot_general(c, t, dims, preferred_element_type=jnp.float32)
    sl = lax.dot_general(c, s, dims, preferred_element_type=jnp.float32)
    a = al_ref[0:1, :]
    logz = al_ref[1:2, :]
    target = rows_all * jnp.exp(tl / teacher_temp) * a * col_ref[...]
    probs = jnp.exp(sl / student_temp - logz)
    g = (scale * (probs - target)).astype(jnp.bfloat16)
    out_ref[...] += jnp.dot(g, s, preferred_element_type=jnp.float32)


def _col_kernel(t_ref, c_ref, a_ref, out_ref):
    dims = (((1,), (1,)), ((), ()))
    w = jnp.exp(
        lax.dot_general(t_ref[...], c_ref[...], dims, preferred_element_type=jnp.float32)
        / teacher_temp
    )
    out_ref[...] = jnp.sum(w * a_ref[...], axis=0, keepdims=True)


def _row_kernel(t_ref, c_ref, col_ref, out_ref):
    @pl.when(pl.program_id(0) == 0)
    def _():
        out_ref[...] = jnp.zeros_like(out_ref)

    dims = (((1,), (1,)), ((), ()))
    w = jnp.exp(
        lax.dot_general(t_ref[...], c_ref[...], dims, preferred_element_type=jnp.float32)
        / teacher_temp
    )
    out_ref[...] += jnp.sum(w * col_ref[...], axis=1, keepdims=True)


def sweep(tn_group, cn, vec, by_column, block=4096):
    rows, width = tn_group.shape
    count = cn.shape[0]
    specs = [
        pl.BlockSpec((rows, width), lambda j: (0, 0)),
        pl.BlockSpec((block, width), lambda j: (j, 0)),
    ]
    if by_column:
        kern, vec = _col_kernel, vec.reshape(rows, 1)
        specs.append(pl.BlockSpec((rows, 1), lambda j: (0, 0)))
        out_spec = pl.BlockSpec((1, block), lambda j: (0, j))
        out_shape = jax.ShapeDtypeStruct((1, count), jnp.float32)
    else:
        kern, vec = _row_kernel, vec.reshape(1, count)
        specs.append(pl.BlockSpec((1, block), lambda j: (0, j)))
        out_spec = pl.BlockSpec((rows, 1), lambda j: (0, 0))
        out_shape = jax.ShapeDtypeStruct((rows, 1), jnp.float32)
    out = pl.pallas_call(
        kern,
        grid=(count // block,),
        in_specs=specs,
        out_specs=out_spec,
        out_shape=out_shape,
        compiler_params=pltpu.CompilerParams(
            dimension_semantics=("arbitrary",), vmem_limit_bytes=56 * 1024 * 1024
        ),
        cost_estimate=pl.CostEstimate(
            flops=2 * rows * count * width,
            transcendentals=rows * count,
            bytes_accessed=2 * (rows + count) * width,
        ),
    )(tn_group, cn, vec)
    return out.reshape(-1)


def protos_grad(ts, c_mine, col_mine, al, rows_all, scale, block=4096, interpret=False):
    n, w2 = ts.shape
    width = w2 // 2
    m = c_mine.shape[0]
    kern = functools.partial(_protos_kernel, rows_all=rows_all, scale=scale, width=width)
    out = pl.pallas_call(
        kern,
        grid=(n // block,),
        in_specs=[
            pl.BlockSpec((block, w2), lambda i: (i, 0)),
            pl.BlockSpec((m, width), lambda i: (0, 0)),
            pl.BlockSpec((m, 1), lambda i: (0, 0)),
            pl.BlockSpec((2, block), lambda i: (0, i)),
        ],
        out_specs=pl.BlockSpec((m, width), lambda i: (0, 0)),
        out_shape=jax.ShapeDtypeStruct((m, width), jnp.float32),
        compiler_params=pltpu.CompilerParams(
            dimension_semantics=("arbitrary",), vmem_limit_bytes=56 * 1024 * 1024
        ),
        cost_estimate=pl.CostEstimate(
            flops=6 * n * m * width,
            transcendentals=2 * n * m,
            bytes_accessed=2 * n * w2 + 4 * m * width,
        ),
        interpret=interpret,
    )(ts, c_mine, col_mine.reshape(m, 1), al)
    return out / student_temp


def side_by_side(arrays, axis, dim, along):
    ends, at = ([], 0)
    for a in arrays[:-1]:
        at += a.shape[along]
        ends.append(at)
    both = jnp.concatenate(arrays, axis=along)
    return tuple(jnp.split(lax.all_gather(both, axis, axis=dim, tiled=True), ends, axis=along))


def cut_along(value, dim, length):
    lengths = value.shape
    parts = value.reshape(*lengths[:dim], length, lengths[dim] // length, *lengths[dim + 1 :])
    return jnp.moveaxis(parts, dim, 0)


def summed_on_arrival(value, axis, dim):
    parts = cut_along(value, dim, lax.axis_size(axis))
    arrived = lax.all_to_all(parts, axis, split_axis=0, concat_axis=0, tiled=True)
    return arrived.sum(axis=0)


def laid_out(parts, dim):
    parts = jnp.moveaxis(parts, 0, dim)
    lengths = parts.shape
    return parts.reshape(*lengths[:dim], lengths[dim] * lengths[dim + 1], *lengths[dim + 2 :])


def copy_for_each(value, axis):
    copies = jnp.broadcast_to(value, (lax.axis_size(axis), *value.shape))
    return lax.all_to_all(copies, axis, split_axis=0, concat_axis=0, tiled=True)


def gather_directly(value, axis, dim):
    return laid_out(copy_for_each(value, axis), dim)


def over_copies(value, axis):
    return copy_for_each(value, axis).sum(axis=0)


def gather_turned(arrays, axis, dims):
    turned = [jnp.moveaxis(a, dim, 0) for a, dim in zip(arrays, dims)]
    widths = [t[0].size for t in turned]
    both = jnp.concatenate([t.reshape(-1, w) for t, w in zip(turned, widths)], axis=1)
    out = lax.all_gather(both, axis, axis=0, tiled=True)
    parts = jnp.split(out, [sum(widths[:k]) for k in range(1, len(widths))], axis=1)
    return tuple(
        (
            jnp.moveaxis(b.reshape(-1, *t.shape[1:]), 0, dim)
            for b, t, dim in zip(parts, turned, dims)
        )
    )


def unit_rows(value):
    full = value.astype(jnp.float32)
    return (
        full
        * lax.rsqrt(jnp.mean(full * full, axis=1, keepdims=True) + 1e-06)
        / math.sqrt(value.shape[1])
    )


def against(left, right):
    return lax.dot_general(
        left, right, (((1,), (1,)), ((), ())), preferred_element_type=jnp.float32
    )


def per_device(teacher, student, prototypes):
    n_proto = lax.axis_size("proto")
    n_batch = lax.axis_size("batch")
    own_rows = teacher.shape[0]
    count_all = prototypes.shape[0] * n_proto
    rows_all = own_rows * n_proto * n_batch
    tn = unit_rows(teacher).astype(jnp.bfloat16)
    sn = unit_rows(student).astype(jnp.bfloat16)
    cn = unit_rows(prototypes).astype(jnp.bfloat16)
    width = tn.shape[1]
    group = gather_directly(jnp.concatenate((tn, sn), axis=1), "proto", 0)
    tn_group, sn_group = group[:, :width], group[:, width:]
    weight = jnp.exp(against(tn_group, cn) / teacher_temp)
    row_scale = jnp.ones((tn_group.shape[0],), jnp.float32)
    col_scale = None
    for step in range(ITERS):
        mass_local = sweep(tn_group, cn, row_scale, True)
        share = summed_on_arrival(mass_local, "batch", 0)
        col_scale = gather_directly(1.0 / (count_all * share), "batch", 0)
        sample_local = sweep(tn_group, cn, col_scale, False)
        row_scale = 1.0 / (rows_all * over_copies(sample_local, "proto"))
    targets = rows_all * weight * row_scale[:, None] * col_scale[None, :]
    logits = against(sn_group, cn) / student_temp
    logz = jnp.log(over_copies(jnp.sum(jnp.exp(logits), axis=1), "proto"))
    logp = logits - logz[:, None]
    scale = 16.0 * math.sqrt(count_all)
    grads = (scale * (jnp.exp(logp) - targets)).astype(jnp.bfloat16)
    sn_partial = jnp.dot(grads, cn, preferred_element_type=jnp.float32) / student_temp
    mine_rows = prototypes.shape[0] // n_batch
    offset = lax.axis_index("batch") * mine_rows
    c_mine = lax.dynamic_slice_in_dim(cn, offset, mine_rows, 0)
    col_mine = lax.dynamic_slice_in_dim(col_scale, offset, mine_rows, 0)
    both = gather_directly(jnp.stack([row_scale, logz], axis=1), "batch", 0)
    sn_partial, both = lax.optimization_barrier((sn_partial, both))
    grad_sn = summed_on_arrival(sn_partial, "proto", 0)
    pieces = lax.all_gather(
        jnp.concatenate((tn_group, sn_group), axis=1), "batch", axis=0, tiled=True
    )
    grad_protos = protos_grad(pieces, c_mine, col_mine, both.T, rows_all, scale)
    _, pull = jax.vjp(unit_rows, student.astype(jnp.float32))
    grad_student = pull(grad_sn)[0]
    return (grad_student, grad_protos)


def solution(mesh):
    return jax.shard_map(
        per_device,
        mesh=mesh,
        in_specs=(P(("proto", "batch"), None), P(("proto", "batch"), None), P("proto", None)),
        out_specs=(P(("proto", "batch"), None), P(("proto", "batch"), None)),
        check_vma=False,
    )
```

```python
import math

import jax
import jax.numpy as jnp
from jax import lax
from jax.sharding import PartitionSpec as P
from jax.experimental import pallas as pl
from jax.experimental.pallas import tpu as pltpu
import functools

ITERS = 3


teacher_temp = 0.05
student_temp = 0.1

def _protos_kernel(ts_ref, c_ref, col_ref, al_ref, out_ref, *, rows_all, scale, width):
    @pl.when(pl.program_id(0) == 0)
    def _():
        out_ref[...] = jnp.zeros_like(out_ref)

    t = ts_ref[:, :width]
    s = ts_ref[:, width:]
    c = c_ref[...]
    dims = (((1,), (1,)), ((), ()))
    tl = lax.dot_general(c, t, dims, preferred_element_type=jnp.float32)
    sl = lax.dot_general(c, s, dims, preferred_element_type=jnp.float32)
    a = al_ref[0:1, :]
    logz = al_ref[1:2, :]
    target = rows_all * jnp.exp(tl / teacher_temp) * a * col_ref[...]
    probs = jnp.exp(sl / student_temp - logz)
    g = (scale * (probs - target)).astype(jnp.bfloat16)
    out_ref[...] += jnp.dot(g, s, preferred_element_type=jnp.float32)


def _col_kernel(t_ref, c_ref, a_ref, out_ref):
    dims = (((1,), (1,)), ((), ()))
    w = jnp.exp(
        lax.dot_general(t_ref[...], c_ref[...], dims, preferred_element_type=jnp.float32)
        / teacher_temp
    )
    out_ref[...] = jnp.sum(w * a_ref[...], axis=0, keepdims=True)


def _row_kernel(t_ref, c_ref, col_ref, out_ref):
    @pl.when(pl.program_id(0) == 0)
    def _():
        out_ref[...] = jnp.zeros_like(out_ref)

    dims = (((1,), (1,)), ((), ()))
    w = jnp.exp(
        lax.dot_general(t_ref[...], c_ref[...], dims, preferred_element_type=jnp.float32)
        / teacher_temp
    )
    out_ref[...] += jnp.sum(w * col_ref[...], axis=1, keepdims=True)


def sweep(tn_group, cn, vec, by_column, block=4096):
    rows, width = tn_group.shape
    count = cn.shape[0]
    specs = [
        pl.BlockSpec((rows, width), lambda j: (0, 0)),
        pl.BlockSpec((block, width), lambda j: (j, 0)),
    ]
    if by_column:
        kern, vec = _col_kernel, vec.reshape(rows, 1)
        specs.append(pl.BlockSpec((rows, 1), lambda j: (0, 0)))
        out_spec = pl.BlockSpec((1, block), lambda j: (0, j))
        out_shape = jax.ShapeDtypeStruct((1, count), jnp.float32)
    else:
        kern, vec = _row_kernel, vec.reshape(1, count)
        specs.append(pl.BlockSpec((1, block), lambda j: (0, j)))
        out_spec = pl.BlockSpec((rows, 1), lambda j: (0, 0))
        out_shape = jax.ShapeDtypeStruct((rows, 1), jnp.float32)
    out = pl.pallas_call(
        kern,
        grid=(count // block,),
        in_specs=specs,
        out_specs=out_spec,
        out_shape=out_shape,
        compiler_params=pltpu.CompilerParams(
            dimension_semantics=("arbitrary",), vmem_limit_bytes=56 * 1024 * 1024
        ),
        cost_estimate=pl.CostEstimate(
            flops=2 * rows * count * width,
            transcendentals=rows * count,
            bytes_accessed=2 * (rows + count) * width,
        ),
    )(tn_group, cn, vec)
    return out.reshape(-1)


def protos_grad(ts, c_mine, col_mine, al, rows_all, scale, block=4096, interpret=False):
    n, w2 = ts.shape
    width = w2 // 2
    m = c_mine.shape[0]
    kern = functools.partial(_protos_kernel, rows_all=rows_all, scale=scale, width=width)
    out = pl.pallas_call(
        kern,
        grid=(n // block,),
        in_specs=[
            pl.BlockSpec((block, w2), lambda i: (i, 0)),
            pl.BlockSpec((m, width), lambda i: (0, 0)),
            pl.BlockSpec((m, 1), lambda i: (0, 0)),
            pl.BlockSpec((2, block), lambda i: (0, i)),
        ],
        out_specs=pl.BlockSpec((m, width), lambda i: (0, 0)),
        out_shape=jax.ShapeDtypeStruct((m, width), jnp.float32),
        compiler_params=pltpu.CompilerParams(
            dimension_semantics=("arbitrary",), vmem_limit_bytes=56 * 1024 * 1024
        ),
        cost_estimate=pl.CostEstimate(
            flops=6 * n * m * width,
            transcendentals=2 * n * m,
            bytes_accessed=2 * n * w2 + 4 * m * width,
        ),
        interpret=interpret,
    )(ts, c_mine, col_mine.reshape(m, 1), al)
    return out / student_temp


def side_by_side(arrays, axis, dim, along):
    ends, at = ([], 0)
    for a in arrays[:-1]:
        at += a.shape[along]
        ends.append(at)
    both = jnp.concatenate(arrays, axis=along)
    return tuple(jnp.split(lax.all_gather(both, axis, axis=dim, tiled=True), ends, axis=along))


def cut_along(value, dim, length):
    lengths = value.shape
    parts = value.reshape(*lengths[:dim], length, lengths[dim] // length, *lengths[dim + 1 :])
    return jnp.moveaxis(parts, dim, 0)


def summed_on_arrival(value, axis, dim):
    parts = cut_along(value, dim, lax.axis_size(axis))
    arrived = lax.all_to_all(parts, axis, split_axis=0, concat_axis=0, tiled=True)
    return arrived.sum(axis=0)


def laid_out(parts, dim):
    parts = jnp.moveaxis(parts, 0, dim)
    lengths = parts.shape
    return parts.reshape(*lengths[:dim], lengths[dim] * lengths[dim + 1], *lengths[dim + 2 :])


def copy_for_each(value, axis):
    copies = jnp.broadcast_to(value, (lax.axis_size(axis), *value.shape))
    return lax.all_to_all(copies, axis, split_axis=0, concat_axis=0, tiled=True)


def gather_directly(value, axis, dim):
    return laid_out(copy_for_each(value, axis), dim)


def over_copies(value, axis):
    return copy_for_each(value, axis).sum(axis=0)


def gather_turned(arrays, axis, dims):
    turned = [jnp.moveaxis(a, dim, 0) for a, dim in zip(arrays, dims)]
    widths = [t[0].size for t in turned]
    both = jnp.concatenate([t.reshape(-1, w) for t, w in zip(turned, widths)], axis=1)
    out = lax.all_gather(both, axis, axis=0, tiled=True)
    parts = jnp.split(out, [sum(widths[:k]) for k in range(1, len(widths))], axis=1)
    return tuple(
        (
            jnp.moveaxis(b.reshape(-1, *t.shape[1:]), 0, dim)
            for b, t, dim in zip(parts, turned, dims)
        )
    )


def unit_rows(value):
    full = value.astype(jnp.float32)
    return (
        full
        * lax.rsqrt(jnp.mean(full * full, axis=1, keepdims=True) + 1e-06)
        / math.sqrt(value.shape[1])
    )


def against(left, right):
    return lax.dot_general(
        left, right, (((1,), (1,)), ((), ())), preferred_element_type=jnp.float32
    )


def per_device(teacher, student, prototypes):
    n_proto = lax.axis_size("proto")
    n_batch = lax.axis_size("batch")
    own_rows = teacher.shape[0]
    count_all = prototypes.shape[0] * n_proto
    rows_all = own_rows * n_proto * n_batch
    tn = unit_rows(teacher).astype(jnp.bfloat16)
    sn = unit_rows(student).astype(jnp.bfloat16)
    cn = unit_rows(prototypes).astype(jnp.bfloat16)
    width = tn.shape[1]
    group = gather_directly(jnp.concatenate((tn, sn), axis=1), "proto", 0)
    tn_group, sn_group = group[:, :width], group[:, width:]
    weight = jnp.exp(against(tn_group, cn) / teacher_temp)
    row_scale = jnp.ones((tn_group.shape[0],), jnp.float32)
    col_scale = None
    for step in range(ITERS):
        mass_local = sweep(tn_group, cn, row_scale, True)
        share = summed_on_arrival(mass_local, "batch", 0)
        col_scale = gather_directly(1.0 / (count_all * share), "batch", 0)
        sample_local = sweep(tn_group, cn, col_scale, False)
        row_scale = 1.0 / (rows_all * over_copies(sample_local, "proto"))
    targets = rows_all * weight * row_scale[:, None] * col_scale[None, :]
    logits = against(sn_group, cn) / student_temp
    logz = jnp.log(over_copies(jnp.sum(jnp.exp(logits), axis=1), "proto"))
    logp = logits - logz[:, None]
    scale = 16.0 * math.sqrt(count_all)
    grads = (scale * (jnp.exp(logp) - targets)).astype(jnp.bfloat16)
    sn_partial = jnp.dot(grads, cn, preferred_element_type=jnp.float32) / student_temp
    mine_rows = prototypes.shape[0] // n_batch
    offset = lax.axis_index("batch") * mine_rows
    c_mine = lax.dynamic_slice_in_dim(cn, offset, mine_rows, 0)
    col_mine = lax.dynamic_slice_in_dim(col_scale, offset, mine_rows, 0)
    both = gather_directly(jnp.stack([row_scale, logz], axis=1), "batch", 0)
    sn_partial, both = lax.optimization_barrier((sn_partial, both))
    pieces = lax.all_gather(
        jnp.concatenate((tn_group, sn_group), axis=1), "batch", axis=0, tiled=True
    )
    sn_partial, pieces = lax.optimization_barrier((sn_partial, pieces))
    grad_sn = lax.psum_scatter(sn_partial, "proto", scatter_dimension=0, tiled=True)
    grad_protos = protos_grad(pieces, c_mine, col_mine, both.T, rows_all, scale)
    _, pull = jax.vjp(unit_rows, student.astype(jnp.float32))
    grad_student = pull(grad_sn)[0]
    return (grad_student, grad_protos)


def solution(mesh):
    return jax.shard_map(
        per_device,
        mesh=mesh,
        in_specs=(P(("proto", "batch"), None), P(("proto", "batch"), None), P("proto", None)),
        out_specs=(P(("proto", "batch"), None), P(("proto", "batch"), None)),
        check_vma=False,
    )
```

```python
import math

import jax
import jax.numpy as jnp
from jax import lax
from jax.sharding import PartitionSpec as P
from jax.experimental import pallas as pl
from jax.experimental.pallas import tpu as pltpu
import functools

ITERS = 3


teacher_temp = 0.05
student_temp = 0.1

def _protos_kernel(ts_ref, c_ref, col_ref, al_ref, out_ref, *, rows_all, scale, width):
    @pl.when(pl.program_id(0) == 0)
    def _():
        out_ref[...] = jnp.zeros_like(out_ref)

    t = ts_ref[:, :width]
    s = ts_ref[:, width:]
    c = c_ref[...]
    dims = (((1,), (1,)), ((), ()))
    tl = lax.dot_general(c, t, dims, preferred_element_type=jnp.float32)
    sl = lax.dot_general(c, s, dims, preferred_element_type=jnp.float32)
    a = al_ref[0:1, :]
    logz = al_ref[1:2, :]
    target = rows_all * jnp.exp(tl / teacher_temp) * a * col_ref[...]
    probs = jnp.exp(sl / student_temp - logz)
    g = (scale * (probs - target)).astype(jnp.bfloat16)
    out_ref[...] += jnp.dot(g, s, preferred_element_type=jnp.float32)


def _col_kernel(t_ref, c_ref, a_ref, out_ref):
    dims = (((1,), (1,)), ((), ()))
    w = jnp.exp(
        lax.dot_general(t_ref[...], c_ref[...], dims, preferred_element_type=jnp.float32)
        / teacher_temp
    )
    out_ref[...] = jnp.sum(w * a_ref[...], axis=0, keepdims=True)


def _row_kernel(t_ref, c_ref, col_ref, out_ref):
    @pl.when(pl.program_id(0) == 0)
    def _():
        out_ref[...] = jnp.zeros_like(out_ref)

    dims = (((1,), (1,)), ((), ()))
    w = jnp.exp(
        lax.dot_general(t_ref[...], c_ref[...], dims, preferred_element_type=jnp.float32)
        / teacher_temp
    )
    out_ref[...] += jnp.sum(w * col_ref[...], axis=1, keepdims=True)


def sweep(tn_group, cn, vec, by_column, block=2048):
    rows, width = tn_group.shape
    count = cn.shape[0]
    specs = [
        pl.BlockSpec((rows, width), lambda j: (0, 0)),
        pl.BlockSpec((block, width), lambda j: (j, 0)),
    ]
    if by_column:
        kern, vec = _col_kernel, vec.reshape(rows, 1)
        specs.append(pl.BlockSpec((rows, 1), lambda j: (0, 0)))
        out_spec = pl.BlockSpec((1, block), lambda j: (0, j))
        out_shape = jax.ShapeDtypeStruct((1, count), jnp.float32)
    else:
        kern, vec = _row_kernel, vec.reshape(1, count)
        specs.append(pl.BlockSpec((1, block), lambda j: (0, j)))
        out_spec = pl.BlockSpec((rows, 1), lambda j: (0, 0))
        out_shape = jax.ShapeDtypeStruct((rows, 1), jnp.float32)
    out = pl.pallas_call(
        kern,
        grid=(count // block,),
        in_specs=specs,
        out_specs=out_spec,
        out_shape=out_shape,
        compiler_params=pltpu.CompilerParams(
            dimension_semantics=("arbitrary",), vmem_limit_bytes=56 * 1024 * 1024
        ),
        cost_estimate=pl.CostEstimate(
            flops=2 * rows * count * width,
            transcendentals=rows * count,
            bytes_accessed=2 * (rows + count) * width,
        ),
    )(tn_group, cn, vec)
    return out.reshape(-1)


def protos_grad(ts, c_mine, col_mine, al, rows_all, scale, block=4096, interpret=False):
    n, w2 = ts.shape
    width = w2 // 2
    m = c_mine.shape[0]
    kern = functools.partial(_protos_kernel, rows_all=rows_all, scale=scale, width=width)
    out = pl.pallas_call(
        kern,
        grid=(n // block,),
        in_specs=[
            pl.BlockSpec((block, w2), lambda i: (i, 0)),
            pl.BlockSpec((m, width), lambda i: (0, 0)),
            pl.BlockSpec((m, 1), lambda i: (0, 0)),
            pl.BlockSpec((2, block), lambda i: (0, i)),
        ],
        out_specs=pl.BlockSpec((m, width), lambda i: (0, 0)),
        out_shape=jax.ShapeDtypeStruct((m, width), jnp.float32),
        compiler_params=pltpu.CompilerParams(
            dimension_semantics=("arbitrary",), vmem_limit_bytes=56 * 1024 * 1024
        ),
        cost_estimate=pl.CostEstimate(
            flops=6 * n * m * width,
            transcendentals=2 * n * m,
            bytes_accessed=2 * n * w2 + 4 * m * width,
        ),
        interpret=interpret,
    )(ts, c_mine, col_mine.reshape(m, 1), al)
    return out / student_temp


def side_by_side(arrays, axis, dim, along):
    ends, at = ([], 0)
    for a in arrays[:-1]:
        at += a.shape[along]
        ends.append(at)
    both = jnp.concatenate(arrays, axis=along)
    return tuple(jnp.split(lax.all_gather(both, axis, axis=dim, tiled=True), ends, axis=along))


def cut_along(value, dim, length):
    lengths = value.shape
    parts = value.reshape(*lengths[:dim], length, lengths[dim] // length, *lengths[dim + 1 :])
    return jnp.moveaxis(parts, dim, 0)


def summed_on_arrival(value, axis, dim):
    parts = cut_along(value, dim, lax.axis_size(axis))
    arrived = lax.all_to_all(parts, axis, split_axis=0, concat_axis=0, tiled=True)
    return arrived.sum(axis=0)


def laid_out(parts, dim):
    parts = jnp.moveaxis(parts, 0, dim)
    lengths = parts.shape
    return parts.reshape(*lengths[:dim], lengths[dim] * lengths[dim + 1], *lengths[dim + 2 :])


def copy_for_each(value, axis):
    copies = jnp.broadcast_to(value, (lax.axis_size(axis), *value.shape))
    return lax.all_to_all(copies, axis, split_axis=0, concat_axis=0, tiled=True)


def gather_directly(value, axis, dim):
    return laid_out(copy_for_each(value, axis), dim)


def over_copies(value, axis):
    return copy_for_each(value, axis).sum(axis=0)


def gather_turned(arrays, axis, dims):
    turned = [jnp.moveaxis(a, dim, 0) for a, dim in zip(arrays, dims)]
    widths = [t[0].size for t in turned]
    both = jnp.concatenate([t.reshape(-1, w) for t, w in zip(turned, widths)], axis=1)
    out = lax.all_gather(both, axis, axis=0, tiled=True)
    parts = jnp.split(out, [sum(widths[:k]) for k in range(1, len(widths))], axis=1)
    return tuple(
        (
            jnp.moveaxis(b.reshape(-1, *t.shape[1:]), 0, dim)
            for b, t, dim in zip(parts, turned, dims)
        )
    )


def unit_rows(value):
    full = value.astype(jnp.float32)
    return (
        full
        * lax.rsqrt(jnp.mean(full * full, axis=1, keepdims=True) + 1e-06)
        / math.sqrt(value.shape[1])
    )


def against(left, right):
    return lax.dot_general(
        left, right, (((1,), (1,)), ((), ())), preferred_element_type=jnp.float32
    )


def per_device(teacher, student, prototypes):
    n_proto = lax.axis_size("proto")
    n_batch = lax.axis_size("batch")
    own_rows = teacher.shape[0]
    count_all = prototypes.shape[0] * n_proto
    rows_all = own_rows * n_proto * n_batch
    tn = unit_rows(teacher).astype(jnp.bfloat16)
    sn = unit_rows(student).astype(jnp.bfloat16)
    cn = unit_rows(prototypes).astype(jnp.bfloat16)
    width = tn.shape[1]
    group = gather_directly(jnp.concatenate((tn, sn), axis=1), "proto", 0)
    tn_group, sn_group = group[:, :width], group[:, width:]
    weight = jnp.exp(against(tn_group, cn) / teacher_temp)
    row_scale = jnp.ones((tn_group.shape[0],), jnp.float32)
    col_scale = None
    for step in range(ITERS):
        mass_local = sweep(tn_group, cn, row_scale, True)
        share = summed_on_arrival(mass_local, "batch", 0)
        col_scale = gather_directly(1.0 / (count_all * share), "batch", 0)
        sample_local = sweep(tn_group, cn, col_scale, False)
        row_scale = 1.0 / (rows_all * over_copies(sample_local, "proto"))
    targets = rows_all * weight * row_scale[:, None] * col_scale[None, :]
    logits = against(sn_group, cn) / student_temp
    logz = jnp.log(over_copies(jnp.sum(jnp.exp(logits), axis=1), "proto"))
    logp = logits - logz[:, None]
    scale = 16.0 * math.sqrt(count_all)
    grads = (scale * (jnp.exp(logp) - targets)).astype(jnp.bfloat16)
    sn_partial = jnp.dot(grads, cn, preferred_element_type=jnp.float32) / student_temp
    mine_rows = prototypes.shape[0] // n_batch
    offset = lax.axis_index("batch") * mine_rows
    c_mine = lax.dynamic_slice_in_dim(cn, offset, mine_rows, 0)
    col_mine = lax.dynamic_slice_in_dim(col_scale, offset, mine_rows, 0)
    both = gather_directly(jnp.stack([row_scale, logz], axis=1), "batch", 0)
    sn_partial, both = lax.optimization_barrier((sn_partial, both))
    pieces = lax.all_gather(
        jnp.concatenate((tn_group, sn_group), axis=1), "batch", axis=0, tiled=True
    )
    sn_partial, pieces = lax.optimization_barrier((sn_partial, pieces))
    grad_sn = lax.psum_scatter(sn_partial, "proto", scatter_dimension=0, tiled=True)
    grad_protos = protos_grad(pieces, c_mine, col_mine, both.T, rows_all, scale)
    _, pull = jax.vjp(unit_rows, student.astype(jnp.float32))
    grad_student = pull(grad_sn)[0]
    return (grad_student, grad_protos)


def solution(mesh):
    return jax.shard_map(
        per_device,
        mesh=mesh,
        in_specs=(P(("proto", "batch"), None), P(("proto", "batch"), None), P("proto", None)),
        out_specs=(P(("proto", "batch"), None), P(("proto", "batch"), None)),
        check_vma=False,
    )
```

```python
import math

import jax
import jax.numpy as jnp
from jax import lax
from jax.sharding import PartitionSpec as P
from jax.experimental import pallas as pl
from jax.experimental.pallas import tpu as pltpu
import functools

ITERS = 3


teacher_temp = 0.05
student_temp = 0.1

def _protos_kernel(ts_ref, c_ref, col_ref, al_ref, out_ref, *, rows_all, scale, width):
    @pl.when(pl.program_id(0) == 0)
    def _():
        out_ref[...] = jnp.zeros_like(out_ref)

    t = ts_ref[:, :width]
    s = ts_ref[:, width:]
    c = c_ref[...]
    dims = (((1,), (1,)), ((), ()))
    tl = lax.dot_general(c, t, dims, preferred_element_type=jnp.float32)
    sl = lax.dot_general(c, s, dims, preferred_element_type=jnp.float32)
    a = al_ref[0:1, :]
    logz = al_ref[1:2, :]
    target = rows_all * jnp.exp(tl / teacher_temp) * a * col_ref[...]
    probs = jnp.exp(sl / student_temp - logz)
    g = (scale * (probs - target)).astype(jnp.bfloat16)
    out_ref[...] += jnp.dot(g, s, preferred_element_type=jnp.float32)


def _col_kernel(t_ref, c_ref, a_ref, out_ref):
    dims = (((1,), (1,)), ((), ()))
    w = jnp.exp(
        lax.dot_general(t_ref[...], c_ref[...], dims, preferred_element_type=jnp.float32)
        / teacher_temp
    )
    out_ref[...] = jnp.sum(w * a_ref[...], axis=0, keepdims=True)


def _row_kernel(t_ref, c_ref, col_ref, out_ref):
    @pl.when(pl.program_id(0) == 0)
    def _():
        out_ref[...] = jnp.zeros_like(out_ref)

    dims = (((1,), (1,)), ((), ()))
    w = jnp.exp(
        lax.dot_general(t_ref[...], c_ref[...], dims, preferred_element_type=jnp.float32)
        / teacher_temp
    )
    out_ref[...] += jnp.sum(w * col_ref[...], axis=1, keepdims=True)


def sweep(tn_group, cn, vec, by_column, block=4096):
    rows, width = tn_group.shape
    count = cn.shape[0]
    specs = [
        pl.BlockSpec((rows, width), lambda j: (0, 0)),
        pl.BlockSpec((block, width), lambda j: (j, 0)),
    ]
    if by_column:
        kern, vec = _col_kernel, vec.reshape(rows, 1)
        specs.append(pl.BlockSpec((rows, 1), lambda j: (0, 0)))
        out_spec = pl.BlockSpec((1, block), lambda j: (0, j))
        out_shape = jax.ShapeDtypeStruct((1, count), jnp.float32)
    else:
        kern, vec = _row_kernel, vec.reshape(1, count)
        specs.append(pl.BlockSpec((1, block), lambda j: (0, j)))
        out_spec = pl.BlockSpec((rows, 1), lambda j: (0, 0))
        out_shape = jax.ShapeDtypeStruct((rows, 1), jnp.float32)
    out = pl.pallas_call(
        kern,
        grid=(count // block,),
        in_specs=specs,
        out_specs=out_spec,
        out_shape=out_shape,
        compiler_params=pltpu.CompilerParams(
            dimension_semantics=("arbitrary",), vmem_limit_bytes=56 * 1024 * 1024
        ),
        cost_estimate=pl.CostEstimate(
            flops=2 * rows * count * width,
            transcendentals=rows * count,
            bytes_accessed=2 * (rows + count) * width,
        ),
    )(tn_group, cn, vec)
    return out.reshape(-1)


def protos_grad(ts, c_mine, col_mine, al, rows_all, scale, block=8192, interpret=False):
    n, w2 = ts.shape
    width = w2 // 2
    m = c_mine.shape[0]
    kern = functools.partial(_protos_kernel, rows_all=rows_all, scale=scale, width=width)
    out = pl.pallas_call(
        kern,
        grid=(n // block,),
        in_specs=[
            pl.BlockSpec((block, w2), lambda i: (i, 0)),
            pl.BlockSpec((m, width), lambda i: (0, 0)),
            pl.BlockSpec((m, 1), lambda i: (0, 0)),
            pl.BlockSpec((2, block), lambda i: (0, i)),
        ],
        out_specs=pl.BlockSpec((m, width), lambda i: (0, 0)),
        out_shape=jax.ShapeDtypeStruct((m, width), jnp.float32),
        compiler_params=pltpu.CompilerParams(
            dimension_semantics=("arbitrary",), vmem_limit_bytes=56 * 1024 * 1024
        ),
        cost_estimate=pl.CostEstimate(
            flops=6 * n * m * width,
            transcendentals=2 * n * m,
            bytes_accessed=2 * n * w2 + 4 * m * width,
        ),
        interpret=interpret,
    )(ts, c_mine, col_mine.reshape(m, 1), al)
    return out / student_temp


def side_by_side(arrays, axis, dim, along):
    ends, at = ([], 0)
    for a in arrays[:-1]:
        at += a.shape[along]
        ends.append(at)
    both = jnp.concatenate(arrays, axis=along)
    return tuple(jnp.split(lax.all_gather(both, axis, axis=dim, tiled=True), ends, axis=along))


def cut_along(value, dim, length):
    lengths = value.shape
    parts = value.reshape(*lengths[:dim], length, lengths[dim] // length, *lengths[dim + 1 :])
    return jnp.moveaxis(parts, dim, 0)


def summed_on_arrival(value, axis, dim):
    parts = cut_along(value, dim, lax.axis_size(axis))
    arrived = lax.all_to_all(parts, axis, split_axis=0, concat_axis=0, tiled=True)
    return arrived.sum(axis=0)


def laid_out(parts, dim):
    parts = jnp.moveaxis(parts, 0, dim)
    lengths = parts.shape
    return parts.reshape(*lengths[:dim], lengths[dim] * lengths[dim + 1], *lengths[dim + 2 :])


def copy_for_each(value, axis):
    copies = jnp.broadcast_to(value, (lax.axis_size(axis), *value.shape))
    return lax.all_to_all(copies, axis, split_axis=0, concat_axis=0, tiled=True)


def gather_directly(value, axis, dim):
    return laid_out(copy_for_each(value, axis), dim)


def over_copies(value, axis):
    return copy_for_each(value, axis).sum(axis=0)


def gather_turned(arrays, axis, dims):
    turned = [jnp.moveaxis(a, dim, 0) for a, dim in zip(arrays, dims)]
    widths = [t[0].size for t in turned]
    both = jnp.concatenate([t.reshape(-1, w) for t, w in zip(turned, widths)], axis=1)
    out = lax.all_gather(both, axis, axis=0, tiled=True)
    parts = jnp.split(out, [sum(widths[:k]) for k in range(1, len(widths))], axis=1)
    return tuple(
        (
            jnp.moveaxis(b.reshape(-1, *t.shape[1:]), 0, dim)
            for b, t, dim in zip(parts, turned, dims)
        )
    )


def unit_rows(value):
    full = value.astype(jnp.float32)
    return (
        full
        * lax.rsqrt(jnp.mean(full * full, axis=1, keepdims=True) + 1e-06)
        / math.sqrt(value.shape[1])
    )


def against(left, right):
    return lax.dot_general(
        left, right, (((1,), (1,)), ((), ())), preferred_element_type=jnp.float32
    )


def per_device(teacher, student, prototypes):
    n_proto = lax.axis_size("proto")
    n_batch = lax.axis_size("batch")
    own_rows = teacher.shape[0]
    count_all = prototypes.shape[0] * n_proto
    rows_all = own_rows * n_proto * n_batch
    tn = unit_rows(teacher).astype(jnp.bfloat16)
    sn = unit_rows(student).astype(jnp.bfloat16)
    cn = unit_rows(prototypes).astype(jnp.bfloat16)
    width = tn.shape[1]
    group = gather_directly(jnp.concatenate((tn, sn), axis=1), "proto", 0)
    tn_group, sn_group = group[:, :width], group[:, width:]
    weight = jnp.exp(against(tn_group, cn) / teacher_temp)
    row_scale = jnp.ones((tn_group.shape[0],), jnp.float32)
    col_scale = None
    for step in range(ITERS):
        mass_local = sweep(tn_group, cn, row_scale, True)
        share = summed_on_arrival(mass_local, "batch", 0)
        col_scale = gather_directly(1.0 / (count_all * share), "batch", 0)
        sample_local = sweep(tn_group, cn, col_scale, False)
        row_scale = 1.0 / (rows_all * over_copies(sample_local, "proto"))
    targets = rows_all * weight * row_scale[:, None] * col_scale[None, :]
    logits = against(sn_group, cn) / student_temp
    logz = jnp.log(over_copies(jnp.sum(jnp.exp(logits), axis=1), "proto"))
    logp = logits - logz[:, None]
    scale = 16.0 * math.sqrt(count_all)
    grads = (scale * (jnp.exp(logp) - targets)).astype(jnp.bfloat16)
    sn_partial = jnp.dot(grads, cn, preferred_element_type=jnp.float32) / student_temp
    mine_rows = prototypes.shape[0] // n_batch
    offset = lax.axis_index("batch") * mine_rows
    c_mine = lax.dynamic_slice_in_dim(cn, offset, mine_rows, 0)
    col_mine = lax.dynamic_slice_in_dim(col_scale, offset, mine_rows, 0)
    both = gather_directly(jnp.stack([row_scale, logz], axis=1), "batch", 0)
    sn_partial, both = lax.optimization_barrier((sn_partial, both))
    pieces = lax.all_gather(
        jnp.concatenate((tn_group, sn_group), axis=1), "batch", axis=0, tiled=True
    )
    sn_partial, pieces = lax.optimization_barrier((sn_partial, pieces))
    grad_sn = lax.psum_scatter(sn_partial, "proto", scatter_dimension=0, tiled=True)
    grad_protos = protos_grad(pieces, c_mine, col_mine, both.T, rows_all, scale)
    _, pull = jax.vjp(unit_rows, student.astype(jnp.float32))
    grad_student = pull(grad_sn)[0]
    return (grad_student, grad_protos)


def solution(mesh):
    return jax.shard_map(
        per_device,
        mesh=mesh,
        in_specs=(P(("proto", "batch"), None), P(("proto", "batch"), None), P("proto", None)),
        out_specs=(P(("proto", "batch"), None), P(("proto", "batch"), None)),
        check_vma=False,
    )
```

```python
import math

import jax
import jax.numpy as jnp
from jax import lax
from jax.sharding import PartitionSpec as P
from jax.experimental import pallas as pl
from jax.experimental.pallas import tpu as pltpu
import functools

ITERS = 3


teacher_temp = 0.05
student_temp = 0.1

def _protos_kernel(ts_ref, c_ref, col_ref, al_ref, out_ref, *, rows_all, scale, width):
    @pl.when(pl.program_id(0) == 0)
    def _():
        out_ref[...] = jnp.zeros_like(out_ref)

    t = ts_ref[:, :width]
    s = ts_ref[:, width:]
    c = c_ref[...]
    dims = (((1,), (1,)), ((), ()))
    tl = lax.dot_general(c, t, dims, preferred_element_type=jnp.float32)
    sl = lax.dot_general(c, s, dims, preferred_element_type=jnp.float32)
    a = al_ref[0:1, :]
    logz = al_ref[1:2, :]
    target = rows_all * jnp.exp(tl / teacher_temp) * a * col_ref[...]
    probs = jnp.exp(sl / student_temp - logz)
    g = (scale * (probs - target)).astype(jnp.bfloat16)
    out_ref[...] += jnp.dot(g, s, preferred_element_type=jnp.float32)


def _col_kernel(t_ref, c_ref, a_ref, out_ref):
    dims = (((1,), (1,)), ((), ()))
    w = jnp.exp(
        lax.dot_general(t_ref[...], c_ref[...], dims, preferred_element_type=jnp.float32)
        / teacher_temp
    )
    out_ref[...] = jnp.sum(w * a_ref[...], axis=0, keepdims=True)


def _row_kernel(t_ref, c_ref, col_ref, out_ref):
    @pl.when(pl.program_id(0) == 0)
    def _():
        out_ref[...] = jnp.zeros_like(out_ref)

    dims = (((1,), (1,)), ((), ()))
    w = jnp.exp(
        lax.dot_general(t_ref[...], c_ref[...], dims, preferred_element_type=jnp.float32)
        / teacher_temp
    )
    out_ref[...] += jnp.sum(w * col_ref[...], axis=1, keepdims=True)


def sweep(tn_group, cn, vec, by_column, block=8192):
    rows, width = tn_group.shape
    count = cn.shape[0]
    specs = [
        pl.BlockSpec((rows, width), lambda j: (0, 0)),
        pl.BlockSpec((block, width), lambda j: (j, 0)),
    ]
    if by_column:
        kern, vec = _col_kernel, vec.reshape(rows, 1)
        specs.append(pl.BlockSpec((rows, 1), lambda j: (0, 0)))
        out_spec = pl.BlockSpec((1, block), lambda j: (0, j))
        out_shape = jax.ShapeDtypeStruct((1, count), jnp.float32)
    else:
        kern, vec = _row_kernel, vec.reshape(1, count)
        specs.append(pl.BlockSpec((1, block), lambda j: (0, j)))
        out_spec = pl.BlockSpec((rows, 1), lambda j: (0, 0))
        out_shape = jax.ShapeDtypeStruct((rows, 1), jnp.float32)
    out = pl.pallas_call(
        kern,
        grid=(count // block,),
        in_specs=specs,
        out_specs=out_spec,
        out_shape=out_shape,
        compiler_params=pltpu.CompilerParams(
            dimension_semantics=("arbitrary",), vmem_limit_bytes=56 * 1024 * 1024
        ),
        cost_estimate=pl.CostEstimate(
            flops=2 * rows * count * width,
            transcendentals=rows * count,
            bytes_accessed=2 * (rows + count) * width,
        ),
    )(tn_group, cn, vec)
    return out.reshape(-1)


def protos_grad(ts, c_mine, col_mine, al, rows_all, scale, block=8192, interpret=False):
    n, w2 = ts.shape
    width = w2 // 2
    m = c_mine.shape[0]
    kern = functools.partial(_protos_kernel, rows_all=rows_all, scale=scale, width=width)
    out = pl.pallas_call(
        kern,
        grid=(n // block,),
        in_specs=[
            pl.BlockSpec((block, w2), lambda i: (i, 0)),
            pl.BlockSpec((m, width), lambda i: (0, 0)),
            pl.BlockSpec((m, 1), lambda i: (0, 0)),
            pl.BlockSpec((2, block), lambda i: (0, i)),
        ],
        out_specs=pl.BlockSpec((m, width), lambda i: (0, 0)),
        out_shape=jax.ShapeDtypeStruct((m, width), jnp.float32),
        compiler_params=pltpu.CompilerParams(
            dimension_semantics=("arbitrary",), vmem_limit_bytes=56 * 1024 * 1024
        ),
        cost_estimate=pl.CostEstimate(
            flops=6 * n * m * width,
            transcendentals=2 * n * m,
            bytes_accessed=2 * n * w2 + 4 * m * width,
        ),
        interpret=interpret,
    )(ts, c_mine, col_mine.reshape(m, 1), al)
    return out / student_temp


def side_by_side(arrays, axis, dim, along):
    ends, at = ([], 0)
    for a in arrays[:-1]:
        at += a.shape[along]
        ends.append(at)
    both = jnp.concatenate(arrays, axis=along)
    return tuple(jnp.split(lax.all_gather(both, axis, axis=dim, tiled=True), ends, axis=along))


def cut_along(value, dim, length):
    lengths = value.shape
    parts = value.reshape(*lengths[:dim], length, lengths[dim] // length, *lengths[dim + 1 :])
    return jnp.moveaxis(parts, dim, 0)


def summed_on_arrival(value, axis, dim):
    parts = cut_along(value, dim, lax.axis_size(axis))
    arrived = lax.all_to_all(parts, axis, split_axis=0, concat_axis=0, tiled=True)
    return arrived.sum(axis=0)


def laid_out(parts, dim):
    parts = jnp.moveaxis(parts, 0, dim)
    lengths = parts.shape
    return parts.reshape(*lengths[:dim], lengths[dim] * lengths[dim + 1], *lengths[dim + 2 :])


def copy_for_each(value, axis):
    copies = jnp.broadcast_to(value, (lax.axis_size(axis), *value.shape))
    return lax.all_to_all(copies, axis, split_axis=0, concat_axis=0, tiled=True)


def gather_directly(value, axis, dim):
    return laid_out(copy_for_each(value, axis), dim)


def over_copies(value, axis):
    return copy_for_each(value, axis).sum(axis=0)


def gather_turned(arrays, axis, dims):
    turned = [jnp.moveaxis(a, dim, 0) for a, dim in zip(arrays, dims)]
    widths = [t[0].size for t in turned]
    both = jnp.concatenate([t.reshape(-1, w) for t, w in zip(turned, widths)], axis=1)
    out = lax.all_gather(both, axis, axis=0, tiled=True)
    parts = jnp.split(out, [sum(widths[:k]) for k in range(1, len(widths))], axis=1)
    return tuple(
        (
            jnp.moveaxis(b.reshape(-1, *t.shape[1:]), 0, dim)
            for b, t, dim in zip(parts, turned, dims)
        )
    )


def unit_rows(value):
    full = value.astype(jnp.float32)
    return (
        full
        * lax.rsqrt(jnp.mean(full * full, axis=1, keepdims=True) + 1e-06)
        / math.sqrt(value.shape[1])
    )


def against(left, right):
    return lax.dot_general(
        left, right, (((1,), (1,)), ((), ())), preferred_element_type=jnp.float32
    )


def per_device(teacher, student, prototypes):
    n_proto = lax.axis_size("proto")
    n_batch = lax.axis_size("batch")
    own_rows = teacher.shape[0]
    count_all = prototypes.shape[0] * n_proto
    rows_all = own_rows * n_proto * n_batch
    tn = unit_rows(teacher).astype(jnp.bfloat16)
    sn = unit_rows(student).astype(jnp.bfloat16)
    cn = unit_rows(prototypes).astype(jnp.bfloat16)
    width = tn.shape[1]
    group = gather_directly(jnp.concatenate((tn, sn), axis=1), "proto", 0)
    tn_group, sn_group = group[:, :width], group[:, width:]
    weight = jnp.exp(against(tn_group, cn) / teacher_temp)
    row_scale = jnp.ones((tn_group.shape[0],), jnp.float32)
    col_scale = None
    for step in range(ITERS):
        mass_local = sweep(tn_group, cn, row_scale, True)
        share = summed_on_arrival(mass_local, "batch", 0)
        col_scale = gather_directly(1.0 / (count_all * share), "batch", 0)
        sample_local = sweep(tn_group, cn, col_scale, False)
        row_scale = 1.0 / (rows_all * over_copies(sample_local, "proto"))
    targets = rows_all * weight * row_scale[:, None] * col_scale[None, :]
    logits = against(sn_group, cn) / student_temp
    logz = jnp.log(over_copies(jnp.sum(jnp.exp(logits), axis=1), "proto"))
    logp = logits - logz[:, None]
    scale = 16.0 * math.sqrt(count_all)
    grads = (scale * (jnp.exp(logp) - targets)).astype(jnp.bfloat16)
    sn_partial = jnp.dot(grads, cn, preferred_element_type=jnp.float32) / student_temp
    mine_rows = prototypes.shape[0] // n_batch
    offset = lax.axis_index("batch") * mine_rows
    c_mine = lax.dynamic_slice_in_dim(cn, offset, mine_rows, 0)
    col_mine = lax.dynamic_slice_in_dim(col_scale, offset, mine_rows, 0)
    both = gather_directly(jnp.stack([row_scale, logz], axis=1), "batch", 0)
    sn_partial, both = lax.optimization_barrier((sn_partial, both))
    pieces = lax.all_gather(
        jnp.concatenate((tn_group, sn_group), axis=1), "batch", axis=0, tiled=True
    )
    sn_partial, pieces = lax.optimization_barrier((sn_partial, pieces))
    grad_sn = lax.psum_scatter(sn_partial, "proto", scatter_dimension=0, tiled=True)
    grad_protos = protos_grad(pieces, c_mine, col_mine, both.T, rows_all, scale)
    _, pull = jax.vjp(unit_rows, student.astype(jnp.float32))
    grad_student = pull(grad_sn)[0]
    return (grad_student, grad_protos)


def solution(mesh):
    return jax.shard_map(
        per_device,
        mesh=mesh,
        in_specs=(P(("proto", "batch"), None), P(("proto", "batch"), None), P("proto", None)),
        out_specs=(P(("proto", "batch"), None), P(("proto", "batch"), None)),
        check_vma=False,
    )
```
